128 devices in a mesh: row: 4 (over x), col: 2 (over core), layer: 16 (over z, y).
Axes of the slice: x: 4, y: 4, z: 4, core: 2. Of those that a mesh axis runs over, the one named last changes fastest.
Arguments:
- left_blocks: bfloat16 [4, 2, 16, 48, 128, 128], P('row', 'col', 'layer'), may hold values from -0.8984375 to 0.8984375
- left_rows: int32 [4, 2, 16, 48], P('row', 'col', 'layer'), may hold values from 0 to 7
- right_blocks: bfloat16 [4, 2, 16, 48, 128, 128], P('row', 'col', 'layer'), may hold values from -0.8984375 to 0.8984375
- right_cols: int32 [4, 2, 16, 48], P('row', 'col', 'layer'), may hold values from 0 to 31
- pair_left: int32 [4, 2, 16, 4, 192], P('row', 'col', 'layer'), may hold values from 0 to 47
- pair_right: int32 [4, 2, 16, 4, 192], P('row', 'col', 'layer'), may hold values from 0 to 47
- pair_count: int32 [4, 2, 16, 4], P('row', 'col', 'layer'), may hold values from 24 to 192, as said below
Outputs:
- product: float32 [2, 4, 256, 128, 128], P('col', 'row', 'layer')
The draws below stay inside these ranges and needn't reach their ends.
Inputs may be any that keep to these rules, and one draw needn't show every extreme that they name: `pair_count`: for each grid position and layer exactly one piece has 192 pairs and the others at most 48; over all pieces one grid position and layer has at most 336 pairs, and one reaches that number.
All inputs are finite; a program needn't handle non-finite values.
Results may differ from the reference program's by a relative error of at most 0.0003.
Values may be sent and summed in bfloat16 or wider, within the bound.
No kernel may reach another device: no remote copies, remote signals or barrier semaphores. Data moves between devices by JAX's collectives and lax.ppermute only.
A program may use at most 192 MiB of HBM per device.

```python
import jax
import jax.numpy as jnp
from jax import lax

BLOCK = 128
SLAB = 128
ROWS_GROUP = 8
LEFT_CAP = 48
RIGHT_CAP = 48
PAIR_CAP = 192
GRID_ROWS = 4
PIECES = 4
GRID_COLS = 2
LAYERS = 16
SLAB_GROUP = 32


def draw_pair_count(key, part):
    devices_all = GRID_ROWS * GRID_COLS * LAYERS
    key_base, key_hot, key_full = jax.random.split(key, 3)
    base = jax.random.randint(key_base, (devices_all, PIECES), PAIR_CAP // 8, PAIR_CAP // 4 + 1)
    hottest = jax.random.randint(key_hot, (devices_all, 1), 0, PIECES)
    fullest = jax.random.randint(key_full, (), 0, devices_all)
    device_ids = jnp.arange(devices_all)[:, None]
    base = jnp.where(device_ids == fullest, PAIR_CAP // 4, base)
    counts = jnp.where(jnp.arange(PIECES)[None, :] == hottest, PAIR_CAP, base)
    return counts.reshape(GRID_ROWS, GRID_COLS, LAYERS, PIECES).astype(jnp.int32)


def plant(values, stream_key, smallest, high):
    shape = values.shape
    spot = [jax.random.randint(jax.random.fold_in(stream_key, axis), (), 0, shape[axis]) for axis in range(len(shape))]
    values = values.at[tuple(spot)].set(smallest)
    longest = shape.index(max(shape))
    spot[longest] = (spot[longest] + 1) % shape[longest]
    return values.at[tuple(spot)].set(high)


def block_scale(rng, shape, pieces, least, high):
    level, own = 1.0, jax.random.fold_in(rng, 6)
    for dim, parts in pieces:
        heights = jnp.exp(jax.random.uniform(jax.random.fold_in(own, dim), (parts,), jnp.float32, least / len(pieces), high / len(pieces)))
        level = level * jnp.repeat(heights, shape[dim] // parts).reshape([-1 if axis == dim else 1 for axis in range(len(shape))])
    return level


def bell_draw(own_key, extent, deviation, most, pieces=(), kind=jnp.bfloat16):
    level = block_scale(own_key, extent, pieces, -0.22, 0.18) if pieces else 1.0
    values = jax.random.normal(own_key, extent, jnp.float32) * deviation * level
    return jnp.minimum(jnp.maximum(values, -most), most).astype(kind)


def setup_inputs(seed: int = 0) -> dict:
    key_list = jax.random.split(jax.random.key(seed), 8)
    return {
        "left_blocks": bell_draw(key_list[0], (GRID_ROWS, GRID_COLS, LAYERS, LEFT_CAP, BLOCK, BLOCK), 0.15, 0.8984375, ((0, 4), (1, 2), (2, 16))),
        "left_rows": plant(jax.random.randint(key_list[1], (GRID_ROWS, GRID_COLS, LAYERS, LEFT_CAP), 0, ROWS_GROUP), jax.random.fold_in(key_list[1], 1), 0, ROWS_GROUP - 1).astype(jnp.int32),
        "right_blocks": bell_draw(key_list[2], (GRID_ROWS, GRID_COLS, LAYERS, RIGHT_CAP, BLOCK, BLOCK), 0.15, 0.8984375, ((0, 4), (1, 2), (2, 16))),
        "right_cols": plant(jax.random.randint(key_list[3], (GRID_ROWS, GRID_COLS, LAYERS, RIGHT_CAP), 0, SLAB_GROUP), jax.random.fold_in(key_list[3], 1), 0, SLAB_GROUP - 1).astype(jnp.int32),
        "pair_left": plant(jax.random.randint(key_list[4], (GRID_ROWS, GRID_COLS, LAYERS, PIECES, PAIR_CAP), 0, LEFT_CAP), jax.random.fold_in(key_list[4], 1), 0, LEFT_CAP - 1).astype(jnp.int32),
        "pair_right": plant(jax.random.randint(key_list[5], (GRID_ROWS, GRID_COLS, LAYERS, PIECES, PAIR_CAP), 0, RIGHT_CAP), jax.random.fold_in(key_list[5], 1), 0, RIGHT_CAP - 1).astype(jnp.int32),
        "pair_count": draw_pair_count(jax.random.fold_in(key_list[7], 71), 0),
    }


def reference(left_blocks, left_rows, right_blocks, right_cols, pair_left, pair_right, pair_count):
    slab_width = SLAB // GRID_ROWS
    targets = ROWS_GROUP * slab_width
    slot_index = jnp.arange(PAIR_CAP, dtype=jnp.int32)

    def one_position(position):
        row_here = position // GRID_COLS
        col_here = position % GRID_COLS

        def add_piece(totals, flat):
            layer_here = flat // PIECES
            piece_now = flat % PIECES
            left_owner = (piece_now - col_here) % GRID_ROWS
            right_owner = (piece_now - row_here) % GRID_COLS
            left_list = left_blocks[left_owner, col_here, layer_here]
            right_list = right_blocks[row_here, right_owner, layer_here]
            chosen_left = pair_left[row_here, col_here, layer_here, piece_now]
            chosen_right = pair_right[row_here, col_here, layer_here, piece_now]
            active = slot_index < pair_count[row_here, col_here, layer_here, piece_now]
            left_gathered = left_list[chosen_left].astype(jnp.float32)
            right_gathered = right_list[chosen_right].astype(jnp.float32)
            products = jnp.einsum("pij,pjk->pik", left_gathered, right_gathered)
            row_ids = left_rows[left_owner, col_here, layer_here][chosen_left]
            col_ids = right_cols[row_here, right_owner, layer_here][chosen_right]
            target = jnp.where(active, row_ids * slab_width + col_ids, targets).astype(jnp.int32)
            summed = jax.ops.segment_sum(products, target, num_segments=targets + 1)
            return totals + summed[:targets], None

        start = jnp.zeros((targets, BLOCK, BLOCK), jnp.float32)
        totals, unused = lax.scan(add_piece, start, jnp.arange(LAYERS * PIECES, dtype=jnp.int32))
        return totals

    result = lax.map(one_position, jnp.arange(GRID_ROWS * GRID_COLS, dtype=jnp.int32))
    return result.reshape(GRID_ROWS, GRID_COLS, targets, BLOCK, BLOCK).transpose(1, 0, 2, 3, 4)
```

```python
import jax
import jax.numpy as jnp
from jax import lax
from jax.experimental import pallas as pl
from jax.experimental.pallas import tpu as pltpu
from jax.sharding import PartitionSpec as P

SLAB = 128
ROWS_GROUP = 8


def pair_kernel(slots_left, slots_right, counts, left_ids, right_ids, right_pick,
                left_lists, right_lists, totals):
    list_count = left_lists.shape[0]
    slab_width = totals.shape[0] // ROWS_GROUP
    block_size = totals.shape[-1]

    def clear(t, carry):
        totals[t] = jnp.zeros((block_size, block_size), jnp.float32)
        return carry

    lax.fori_loop(0, totals.shape[0], clear, 0)

    for u in range(list_count):
        v = right_pick[u]

        def add_pair(j, carry, u=u, v=v):
            i = slots_left[u, j]
            k = slots_right[u, j]
            t = left_ids[u, i] * slab_width + right_ids[v, k]
            term = jnp.dot(left_lists[u, i], right_lists[v, k],
                           preferred_element_type=jnp.float32)
            totals[t] = totals[t] + term
            return carry

        lax.fori_loop(0, counts[u], add_pair, 0)


def pair_products(slots_left, slots_right, counts, left_ids, right_ids, right_pick,
                  left_lists, right_lists, targets):
    block_size = left_lists.shape[-1]
    smem = pl.BlockSpec(memory_space=pltpu.SMEM)
    vmem = pl.BlockSpec(memory_space=pltpu.VMEM)
    return pl.pallas_call(
        pair_kernel,
        out_shape=jax.ShapeDtypeStruct((targets, block_size, block_size), jnp.float32),
        in_specs=[smem] * 6 + [vmem, vmem],
        out_specs=vmem,
        compiler_params=pltpu.CompilerParams(vmem_limit_bytes=60 * 1024 * 1024),
    )(slots_left, slots_right, counts, left_ids, right_ids, right_pick, left_lists, right_lists)


def on_device(left_blocks, left_rows, right_blocks, right_cols, pair_left, pair_right, pair_count):
    block_size = left_blocks.shape[-1]
    left_cap = left_blocks.shape[3]
    right_cap = right_blocks.shape[3]
    piece_count = lax.axis_size("row")
    col_count = lax.axis_size("col")
    slab_width = SLAB // piece_count
    targets = ROWS_GROUP * slab_width
    row_here = lax.axis_index("row")
    col_here = lax.axis_index("col")
    left_lists = lax.all_gather(left_blocks.reshape(left_cap, block_size, block_size), "row")
    left_ids = lax.all_gather(left_rows.reshape(left_cap), "row")
    right_lists = lax.all_gather(right_blocks.reshape(right_cap, block_size, block_size), "col")
    right_ids = lax.all_gather(right_cols.reshape(right_cap), "col")
    owners = jnp.arange(piece_count, dtype=jnp.int32)
    piece_of = (owners + col_here) % piece_count
    right_pick = (piece_of - row_here) % col_count
    slots_left = jnp.take(pair_left.reshape(piece_count, -1), piece_of, axis=0)
    slots_right = jnp.take(pair_right.reshape(piece_count, -1), piece_of, axis=0)
    counts = jnp.take(pair_count.reshape(piece_count), piece_of, axis=0)
    totals = pair_products(slots_left, slots_right, counts, left_ids, right_ids, right_pick,
                           left_lists, right_lists, targets)
    owned = lax.psum_scatter(totals, "layer", scatter_dimension=0, tiled=True)
    return owned.reshape(1, 1, -1, block_size, block_size)


def solution(mesh):
    in_specs = (
        P("row", "col", "layer", None, None, None),
        P("row", "col", "layer", None),
        P("row", "col", "layer", None, None, None),
        P("row", "col", "layer", None),
        P("row", "col", "layer", None, None),
        P("row", "col", "layer", None, None),
        P("row", "col", "layer", None),
    )
    out_specs = P("col", "row", "layer", None, None)
    return jax.shard_map(
        on_device, mesh=mesh, in_specs=in_specs, out_specs=out_specs, check_vma=False
    )
```

```python
import jax
import jax.numpy as jnp
from jax import lax
from jax.experimental import pallas as pl
from jax.experimental.pallas import tpu as pltpu
from jax.sharding import PartitionSpec as P

SLAB = 128
ROWS_GROUP = 8
UNROLL = 4


def make_pair_kernel(has_start, right_pick):
    def pair_kernel(slots_left, slots_right, counts, left_ids, right_ids, *refs):
        if has_start:
            left_lists, right_lists, start, totals = refs
        else:
            left_lists, right_lists, totals = refs
        list_count = left_lists.shape[0]
        slab_width = totals.shape[0] // ROWS_GROUP
        block_size = totals.shape[-1]

        if has_start:
            totals[...] = start[...]
        else:
            def clear(t, carry):
                totals[t] = jnp.zeros((block_size, block_size), jnp.float32)
                return carry

            lax.fori_loop(0, totals.shape[0], clear, 0)

        for u in range(list_count):
            v = right_pick[u]

            def one_term(j, u=u, v=v):
                i = slots_left[u, j]
                k = slots_right[u, j]
                t = left_ids[u, i] * slab_width + right_ids[v, k]
                term = jnp.dot(left_lists[u, i], right_lists[v, k],
                               preferred_element_type=jnp.float32)
                return t, term

            def add_group(g, carry):
                made = [one_term(g * UNROLL + q) for q in range(UNROLL)]
                for t, term in made:
                    totals[t] = totals[t] + term
                return carry

            def add_single(j, carry):
                t, term = one_term(j)
                totals[t] = totals[t] + term
                return carry

            count = counts[u]
            groups = count // UNROLL
            lax.fori_loop(0, groups, add_group, 0)
            lax.fori_loop(groups * UNROLL, count, add_single, 0)

    return pair_kernel


def pair_products(slots_left, slots_right, counts, left_ids, right_ids,
                  left_lists, right_lists, right_pick, start=None, targets=None):
    block_size = left_lists.shape[-1]
    smem = pl.BlockSpec(memory_space=pltpu.SMEM)
    vmem = pl.BlockSpec(memory_space=pltpu.VMEM)
    operands = [slots_left, slots_right, counts, left_ids, right_ids, left_lists, right_lists]
    if start is not None:
        operands.append(start)
        targets = start.shape[0]
    return pl.pallas_call(
        make_pair_kernel(start is not None, right_pick),
        out_shape=jax.ShapeDtypeStruct((targets, block_size, block_size), jnp.float32),
        in_specs=[smem] * 5 + [vmem] * (len(operands) - 5),
        out_specs=vmem,
        input_output_aliases={7: 0} if start is not None else {},
        compiler_params=pltpu.CompilerParams(vmem_limit_bytes=60 * 1024 * 1024),
    )(*operands)


def shifted(value, axis, steps):
    count = lax.axis_size(axis)
    pairs = [(source, (source + steps) % count) for source in range(count)]
    return lax.ppermute(value, axis, pairs)


def on_device(left_blocks, left_rows, right_blocks, right_cols, pair_left, pair_right, pair_count):
    block_size = left_blocks.shape[-1]
    left_cap = left_blocks.shape[3]
    right_cap = right_blocks.shape[3]
    piece_count = lax.axis_size("row")
    slab_width = SLAB // piece_count
    targets = ROWS_GROUP * slab_width
    row_here = lax.axis_index("row")
    col_here = lax.axis_index("col")
    own_left = (left_blocks.reshape(left_cap, block_size, block_size), left_rows.reshape(left_cap))
    own_right = (right_blocks.reshape(right_cap, block_size, block_size), right_cols.reshape(right_cap))

    from_below = shifted(own_left, "row", 1)
    from_above = shifted(own_left, "row", -1)
    half = left_cap // 2
    far_low = shifted(jax.tree.map(lambda a: a[:half], from_below), "row", 1)
    far_high = shifted(jax.tree.map(lambda a: a[half:], from_above), "row", -1)
    far = jax.tree.map(lambda a, b: jnp.concatenate([a, b]), far_low, far_high)
    other_right = shifted(own_right, "col", 1)

    slots_left_all = pair_left.reshape(piece_count, -1)
    slots_right_all = pair_right.reshape(piece_count, -1)
    counts_all = pair_count.reshape(piece_count)

    def pieces_for(offsets):
        piece = (row_here + col_here + jnp.array(offsets, jnp.int32)) % piece_count
        return (jnp.take(slots_left_all, piece, axis=0), jnp.take(slots_right_all, piece, axis=0),
                jnp.take(counts_all, piece, axis=0))

    sl, sr, cn = pieces_for([0])
    totals = pair_products(sl, sr, cn, own_left[1][None], own_right[1][None],
                           own_left[0][None], own_right[0][None], (0,), targets=targets)
    sl, sr, cn = pieces_for([2, -1, 1])
    left_stack = jnp.stack([far[0], from_below[0], from_above[0]])
    left_id_stack = jnp.stack([far[1], from_below[1], from_above[1]])
    right_stack = jnp.stack([own_right[0], other_right[0]])
    right_id_stack = jnp.stack([own_right[1], other_right[1]])
    totals = pair_products(sl, sr, cn, left_id_stack, right_id_stack,
                           left_stack, right_stack, (0, 1, 1), start=totals)
    owned = lax.psum_scatter(totals, "layer", scatter_dimension=0, tiled=True)
    return owned.reshape(1, 1, -1, block_size, block_size)


def solution(mesh):
    in_specs = (
        P("row", "col", "layer", None, None, None),
        P("row", "col", "layer", None),
        P("row", "col", "layer", None, None, None),
        P("row", "col", "layer", None),
        P("row", "col", "layer", None, None),
        P("row", "col", "layer", None, None),
        P("row", "col", "layer", None),
    )
    out_specs = P("col", "row", "layer", None, None)
    return jax.shard_map(
        on_device, mesh=mesh, in_specs=in_specs, out_specs=out_specs, check_vma=False
    )
```

```python
import jax
import jax.numpy as jnp
from jax import lax
from jax.experimental import pallas as pl
from jax.experimental.pallas import tpu as pltpu
from jax.sharding import PartitionSpec as P

SLAB = 128
ROWS_GROUP = 8
UNROLL = 4


def make_pair_kernel(has_start, right_pick, list_count, right_count):
    def pair_kernel(slots_left, slots_right, counts, left_ids, right_ids, *refs):
        left_lists = refs[:list_count]
        right_lists = refs[list_count:list_count + right_count]
        totals = refs[-1]
        slab_width = totals.shape[0] // ROWS_GROUP
        block_size = totals.shape[-1]

        if has_start:
            totals[...] = refs[-2][...]
        else:
            def clear(t, carry):
                totals[t] = jnp.zeros((block_size, block_size), jnp.float32)
                return carry

            lax.fori_loop(0, totals.shape[0], clear, 0)

        for u in range(list_count):
            v = right_pick[u]
            left_list = left_lists[u]
            right_list = right_lists[v]

            def one_term(j, u=u, v=v, left_list=left_list, right_list=right_list):
                i = slots_left[u, j]
                k = slots_right[u, j]
                t = left_ids[u, i] * slab_width + right_ids[v, k]
                term = jnp.dot(left_list[i], right_list[k], preferred_element_type=jnp.float32)
                return t, term

            def add_group(g, carry, one_term=one_term):
                made = [one_term(g * UNROLL + q) for q in range(UNROLL)]
                for t, term in made:
                    totals[t] = totals[t] + term
                return carry

            def add_single(j, carry, one_term=one_term):
                t, term = one_term(j)
                totals[t] = totals[t] + term
                return carry

            count = counts[u]
            groups = count // UNROLL
            lax.fori_loop(0, groups, add_group, 0)
            lax.fori_loop(groups * UNROLL, count, add_single, 0)

    return pair_kernel


def pair_products(slots_left, slots_right, counts, left_ids, right_ids,
                  left_lists, right_lists, right_pick, start=None, targets=None):
    block_size = left_lists[0].shape[-1]
    smem = pl.BlockSpec(memory_space=pltpu.SMEM)
    vmem = pl.BlockSpec(memory_space=pltpu.VMEM)
    operands = [slots_left, slots_right, counts, left_ids, right_ids, *left_lists, *right_lists]
    if start is not None:
        operands.append(start)
        targets = start.shape[0]
    return pl.pallas_call(
        make_pair_kernel(start is not None, right_pick, len(left_lists), len(right_lists)),
        out_shape=jax.ShapeDtypeStruct((targets, block_size, block_size), jnp.float32),
        in_specs=[smem] * 5 + [vmem] * (len(operands) - 5),
        out_specs=vmem,
        input_output_aliases={len(operands) - 1: 0} if start is not None else {},
        compiler_params=pltpu.CompilerParams(vmem_limit_bytes=60 * 1024 * 1024),
    )(*operands)


def shifted(value, axis, steps):
    count = lax.axis_size(axis)
    pairs = [(source, (source + steps) % count) for source in range(count)]
    return lax.ppermute(value, axis, pairs)


def on_device(left_blocks, left_rows, right_blocks, right_cols, pair_left, pair_right, pair_count):
    block_size = left_blocks.shape[-1]
    left_cap = left_blocks.shape[3]
    right_cap = right_blocks.shape[3]
    piece_count = lax.axis_size("row")
    slab_width = SLAB // piece_count
    targets = ROWS_GROUP * slab_width
    row_here = lax.axis_index("row")
    col_here = lax.axis_index("col")
    own_left = (left_blocks.reshape(left_cap, block_size, block_size), left_rows.reshape(left_cap))
    own_right = (right_blocks.reshape(right_cap, block_size, block_size), right_cols.reshape(right_cap))

    from_below = shifted(own_left, "row", 1)
    from_above = shifted(own_left, "row", -1)
    half = left_cap // 2
    far_low = shifted(jax.tree.map(lambda a: a[:half], from_below), "row", 1)
    far_high = shifted(jax.tree.map(lambda a: a[half:], from_above), "row", -1)
    far = jax.tree.map(lambda a, b: jnp.concatenate([a, b]), far_low, far_high)
    other_right = shifted(own_right, "col", 1)

    slots_left_all = pair_left.reshape(piece_count, -1)
    slots_right_all = pair_right.reshape(piece_count, -1)
    counts_all = pair_count.reshape(piece_count)

    def pieces_for(offsets):
        piece = (row_here + col_here + jnp.array(offsets, jnp.int32)) % piece_count
        return (jnp.take(slots_left_all, piece, axis=0), jnp.take(slots_right_all, piece, axis=0),
                jnp.take(counts_all, piece, axis=0))

    right_lists = (own_right[0], other_right[0])
    right_id_stack = jnp.stack([own_right[1], other_right[1]])
    sl, sr, cn = pieces_for([0])
    totals = pair_products(sl, sr, cn, own_left[1][None], own_right[1][None],
                           (own_left[0],), (own_right[0],), (0,), targets=targets)
    sl, sr, cn = pieces_for([-1, 1])
    totals = pair_products(sl, sr, cn, jnp.stack([from_below[1], from_above[1]]), right_id_stack,
                           (from_below[0], from_above[0]), right_lists, (1, 1), start=totals)
    sl, sr, cn = pieces_for([2])
    totals = pair_products(sl, sr, cn, far[1][None], right_id_stack,
                           (far[0],), right_lists, (0,), start=totals)
    owned = lax.psum_scatter(totals, "layer", scatter_dimension=0, tiled=True)
    return owned.reshape(1, 1, -1, block_size, block_size)


def solution(mesh):
    in_specs = (
        P("row", "col", "layer", None, None, None),
        P("row", "col", "layer", None),
        P("row", "col", "layer", None, None, None),
        P("row", "col", "layer", None),
        P("row", "col", "layer", None, None),
        P("row", "col", "layer", None, None),
        P("row", "col", "layer", None),
    )
    out_specs = P("col", "row", "layer", None, None)
    return jax.shard_map(
        on_device, mesh=mesh, in_specs=in_specs, out_specs=out_specs, check_vma=False
    )
```

```python
import jax
import jax.numpy as jnp
from jax import lax
from jax.experimental import pallas as pl
from jax.experimental.pallas import tpu as pltpu
from jax.sharding import PartitionSpec as P

SLAB = 128
ROWS_GROUP = 8
UNROLL = 4


def placed(t):
    owner = t // 16
    block = t % 16
    quarter = block // 4
    z_o = owner // 4
    y_o = owner % 4
    first = jnp.where(quarter < 2, y_o, z_o)
    second = jnp.where(quarter < 2, z_o, y_o)
    return quarter * 64 + first * 16 + second * 4 + block % 4


def make_pair_kernel(has_start, right_pick, list_count, right_count):
    def pair_kernel(slots_left, slots_right, counts, left_ids, right_ids, *refs):
        left_lists = refs[:list_count]
        right_lists = refs[list_count:list_count + right_count]
        totals = refs[-1]
        slab_width = totals.shape[0] // ROWS_GROUP
        block_size = totals.shape[-1]

        if has_start:
            totals[...] = refs[-2][...]
        else:
            def clear(t, carry):
                totals[t] = jnp.zeros((block_size, block_size), jnp.float32)
                return carry

            lax.fori_loop(0, totals.shape[0], clear, 0)

        for u in range(list_count):
            v = right_pick[u]
            left_list = left_lists[u]
            right_list = right_lists[v]

            def one_term(j, u=u, v=v, left_list=left_list, right_list=right_list):
                i = slots_left[u, j]
                k = slots_right[u, j]
                t = placed(left_ids[u, i] * slab_width + right_ids[v, k])
                term = jnp.dot(left_list[i], right_list[k], preferred_element_type=jnp.float32)
                return t, term

            def add_group(g, carry, one_term=one_term):
                made = [one_term(g * UNROLL + q) for q in range(UNROLL)]
                for t, term in made:
                    totals[t] = totals[t] + term
                return carry

            def add_single(j, carry, one_term=one_term):
                t, term = one_term(j)
                totals[t] = totals[t] + term
                return carry

            count = counts[u]
            groups = count // UNROLL
            lax.fori_loop(0, groups, add_group, 0)
            lax.fori_loop(groups * UNROLL, count, add_single, 0)

    return pair_kernel


def pair_products(slots_left, slots_right, counts, left_ids, right_ids,
                  left_lists, right_lists, right_pick, start=None, targets=None):
    block_size = left_lists[0].shape[-1]
    smem = pl.BlockSpec(memory_space=pltpu.SMEM)
    vmem = pl.BlockSpec(memory_space=pltpu.VMEM)
    operands = [slots_left, slots_right, counts, left_ids, right_ids, *left_lists, *right_lists]
    if start is not None:
        operands.append(start)
        targets = start.shape[0]
    return pl.pallas_call(
        make_pair_kernel(start is not None, right_pick, len(left_lists), len(right_lists)),
        out_shape=jax.ShapeDtypeStruct((targets, block_size, block_size), jnp.float32),
        in_specs=[smem] * 5 + [vmem] * (len(operands) - 5),
        out_specs=vmem,
        input_output_aliases={len(operands) - 1: 0} if start is not None else {},
        compiler_params=pltpu.CompilerParams(vmem_limit_bytes=60 * 1024 * 1024),
    )(*operands)


def shifted(value, axis, steps):
    count = lax.axis_size(axis)
    pairs = [(source, (source + steps) % count) for source in range(count)]
    return lax.ppermute(value, axis, pairs)


def ring_pairs(step_y, step_z):
    return [(z * 4 + y, ((z + step_z) % 4) * 4 + (y + step_y) % 4) for z in range(4) for y in range(4)]


def ring_pass(chunks, here, pairs, sign):
    count = chunks.shape[0]
    acc = lax.dynamic_index_in_dim(chunks, (here - sign) % count, 0, keepdims=False)
    for step in range(count - 1):
        acc = lax.ppermute(acc, "layer", pairs)
        acc = acc + lax.dynamic_index_in_dim(chunks, (here - sign * (step + 2)) % count, 0,
                                             keepdims=False)
    return acc


def ring_reduce_scatter(totals):
    block_size = totals.shape[-1]
    layer_here = lax.axis_index("layer")
    y_here = layer_here % 4
    z_here = layer_here // 4
    routes = [
        ((y_here, ring_pairs(1, 0), 1), (z_here, ring_pairs(0, 1), 1)),
        ((y_here, ring_pairs(-1, 0), -1), (z_here, ring_pairs(0, -1), -1)),
        ((z_here, ring_pairs(0, 1), 1), (y_here, ring_pairs(1, 0), 1)),
        ((z_here, ring_pairs(0, -1), -1), (y_here, ring_pairs(-1, 0), -1)),
    ]
    quarters = totals.reshape(4, 4, 16, block_size, block_size)
    results = []
    for quarter, (first, second) in enumerate(routes):
        part = ring_pass(quarters[quarter], *first)
        part = ring_pass(part.reshape(4, 4, block_size, block_size), *second)
        results.append(part)
    return jnp.concatenate(results)


def on_device(left_blocks, left_rows, right_blocks, right_cols, pair_left, pair_right, pair_count):
    block_size = left_blocks.shape[-1]
    left_cap = left_blocks.shape[3]
    right_cap = right_blocks.shape[3]
    piece_count = lax.axis_size("row")
    slab_width = SLAB // piece_count
    targets = ROWS_GROUP * slab_width
    row_here = lax.axis_index("row")
    col_here = lax.axis_index("col")
    own_left = (left_blocks.reshape(left_cap, block_size, block_size), left_rows.reshape(left_cap))
    own_right = (right_blocks.reshape(right_cap, block_size, block_size), right_cols.reshape(right_cap))

    from_below = shifted(own_left, "row", 1)
    from_above = shifted(own_left, "row", -1)
    half = left_cap // 2
    far_low = shifted(jax.tree.map(lambda a: a[:half], from_below), "row", 1)
    far_high = shifted(jax.tree.map(lambda a: a[half:], from_above), "row", -1)
    far = jax.tree.map(lambda a, b: jnp.concatenate([a, b]), far_low, far_high)
    other_right = shifted(own_right, "col", 1)

    slots_left_all = pair_left.reshape(piece_count, -1)
    slots_right_all = pair_right.reshape(piece_count, -1)
    counts_all = pair_count.reshape(piece_count)

    def pieces_for(offsets):
        piece = (row_here + col_here + jnp.array(offsets, jnp.int32)) % piece_count
        return (jnp.take(slots_left_all, piece, axis=0), jnp.take(slots_right_all, piece, axis=0),
                jnp.take(counts_all, piece, axis=0))

    right_lists = (own_right[0], other_right[0])
    right_id_stack = jnp.stack([own_right[1], other_right[1]])
    sl, sr, cn = pieces_for([0])
    totals = pair_products(sl, sr, cn, own_left[1][None], own_right[1][None],
                           (own_left[0],), (own_right[0],), (0,), targets=targets)
    sl, sr, cn = pieces_for([-1, 1, 2])
    left_id_stack = jnp.stack([from_below[1], from_above[1], far[1]])
    totals = pair_products(sl, sr, cn, left_id_stack, right_id_stack,
                           (from_below[0], from_above[0], far[0]), right_lists, (1, 1, 0),
                           start=totals)
    owned = ring_reduce_scatter(totals)
    return owned.reshape(1, 1, -1, block_size, block_size)


def solution(mesh):
    in_specs = (
        P("row", "col", "layer", None, None, None),
        P("row", "col", "layer", None),
        P("row", "col", "layer", None, None, None),
        P("row", "col", "layer", None),
        P("row", "col", "layer", None, None),
        P("row", "col", "layer", None, None),
        P("row", "col", "layer", None),
    )
    out_specs = P("col", "row", "layer", None, None)
    return jax.shard_map(
        on_device, mesh=mesh, in_specs=in_specs, out_specs=out_specs, check_vma=False
    )
```

```python
import jax
import jax.numpy as jnp
from jax import lax
from jax.experimental import pallas as pl
from jax.experimental.pallas import tpu as pltpu
from jax.sharding import PartitionSpec as P

SLAB = 128
ROWS_GROUP = 8
UNROLL = 4


def make_pair_kernel(has_start, right_pick, list_count, right_count):
    def pair_kernel(slots_left, slots_right, counts, left_ids, right_ids, *refs):
        left_lists = refs[:list_count]
        right_lists = refs[list_count:list_count + right_count]
        totals = refs[-1]
        slab_width = totals.shape[0] // ROWS_GROUP
        block_size = totals.shape[-1]

        if has_start:
            pltpu.sync_copy(refs[-2], totals)
        else:
            def clear(t, carry):
                totals[t] = jnp.zeros((block_size, block_size), jnp.float32)
                return carry

            lax.fori_loop(0, totals.shape[0], clear, 0)

        for u in range(list_count):
            v = right_pick[u]
            left_list = left_lists[u]
            right_list = right_lists[v]

            def one_term(j, u=u, v=v, left_list=left_list, right_list=right_list):
                i = slots_left[u, j]
                k = slots_right[u, j]
                t = left_ids[u, i] * slab_width + right_ids[v, k]
                term = jnp.dot(left_list[i], right_list[k], preferred_element_type=jnp.float32)
                return t, term

            def add_group(g, carry, one_term=one_term):
                made = [one_term(g * UNROLL + q) for q in range(UNROLL)]
                for t, term in made:
                    totals[t] = totals[t] + term
                return carry

            def add_single(j, carry, one_term=one_term):
                t, term = one_term(j)
                totals[t] = totals[t] + term
                return carry

            count = counts[u]
            groups = count // UNROLL
            lax.fori_loop(0, groups, add_group, 0)
            lax.fori_loop(groups * UNROLL, count, add_single, 0)

    return pair_kernel


def pair_products(slots_left, slots_right, counts, left_ids, right_ids,
                  left_lists, right_lists, right_pick, start=None, targets=None):
    block_size = left_lists[0].shape[-1]
    smem = pl.BlockSpec(memory_space=pltpu.SMEM)
    vmem = pl.BlockSpec(memory_space=pltpu.VMEM)
    operands = [slots_left, slots_right, counts, left_ids, right_ids, *left_lists, *right_lists]
    if start is not None:
        operands.append(start)
        targets = start.shape[0]
    return pl.pallas_call(
        make_pair_kernel(start is not None, right_pick, len(left_lists), len(right_lists)),
        out_shape=jax.ShapeDtypeStruct((targets, block_size, block_size), jnp.float32),
        in_specs=[smem] * 5 + [vmem] * (len(left_lists) + len(right_lists))
        + [pl.BlockSpec(memory_space=pl.ANY)] * (start is not None),
        out_specs=vmem,
        compiler_params=pltpu.CompilerParams(vmem_limit_bytes=60 * 1024 * 1024),
    )(*operands)


def shifted(value, axis, steps):
    count = lax.axis_size(axis)
    pairs = [(source, (source + steps) % count) for source in range(count)]
    return lax.ppermute(value, axis, pairs)


def on_device(left_blocks, left_rows, right_blocks, right_cols, pair_left, pair_right, pair_count):
    block_size = left_blocks.shape[-1]
    left_cap = left_blocks.shape[3]
    right_cap = right_blocks.shape[3]
    piece_count = lax.axis_size("row")
    slab_width = SLAB // piece_count
    targets = ROWS_GROUP * slab_width
    row_here = lax.axis_index("row")
    col_here = lax.axis_index("col")
    own_left = (left_blocks.reshape(left_cap, block_size, block_size), left_rows.reshape(left_cap))
    own_right = (right_blocks.reshape(right_cap, block_size, block_size), right_cols.reshape(right_cap))

    from_below = shifted(own_left, "row", 1)
    from_above = shifted(own_left, "row", -1)
    other_right = shifted(own_right, "col", 1)

    slots_left_all = pair_left.reshape(piece_count, -1)
    slots_right_all = pair_right.reshape(piece_count, -1)
    counts_all = pair_count.reshape(piece_count)

    def pieces_for(offsets):
        piece = (row_here + col_here + jnp.array(offsets, jnp.int32)) % piece_count
        return (jnp.take(slots_left_all, piece, axis=0), jnp.take(slots_right_all, piece, axis=0),
                jnp.take(counts_all, piece, axis=0))

    right_lists = (own_right[0], other_right[0])
    right_id_stack = jnp.stack([own_right[1], other_right[1]])
    sl, sr, cn = pieces_for([0])
    totals = pair_products(sl, sr, cn, own_left[1][None], own_right[1][None],
                           (own_left[0],), (own_right[0],), (0,), targets=targets)
    totals, from_below, from_above = lax.optimization_barrier((totals, from_below, from_above))
    half = left_cap // 2
    far_low = shifted(jax.tree.map(lambda a: a[:half], from_below), "row", 1)
    far_high = shifted(jax.tree.map(lambda a: a[half:], from_above), "row", -1)
    sl, sr, cn = pieces_for([-1, 1, 2])
    far = jax.tree.map(lambda a, b: jnp.concatenate([a, b]), far_low, far_high)
    left_id_stack = jnp.stack([from_below[1], from_above[1], far[1]])
    totals = pair_products(sl, sr, cn, left_id_stack, right_id_stack,
                           (from_below[0], from_above[0], far[0]), right_lists, (1, 1, 0),
                           start=totals)
    owned = lax.psum_scatter(totals, "layer", scatter_dimension=0, tiled=True)
    return owned.reshape(1, 1, -1, block_size, block_size)


def solution(mesh):
    in_specs = (
        P("row", "col", "layer", None, None, None),
        P("row", "col", "layer", None),
        P("row", "col", "layer", None, None, None),
        P("row", "col", "layer", None),
        P("row", "col", "layer", None, None),
        P("row", "col", "layer", None, None),
        P("row", "col", "layer", None),
    )
    out_specs = P("col", "row", "layer", None, None)
    return jax.shard_map(
        on_device, mesh=mesh, in_specs=in_specs, out_specs=out_specs, check_vma=False
    )
```

```python
import jax
import jax.numpy as jnp
from jax import lax
from jax.experimental import pallas as pl
from jax.experimental.pallas import tpu as pltpu
from jax.sharding import PartitionSpec as P

SLAB = 128
ROWS_GROUP = 8
UNROLL = 4
parts = 2


def placed(t, parts):
    owner = t // 16
    block = t % 16
    width = 16 // parts
    return (block // width) * (16 * width) + owner * width + block % width


def make_pair_kernel(has_start, right_pick, list_count, right_count):
    def pair_kernel(slots_left, slots_right, counts, left_ids, right_ids, *refs):
        left_lists = refs[:list_count]
        right_lists = refs[list_count:list_count + right_count]
        totals = refs[-1]
        slab_width = totals.shape[0] // ROWS_GROUP
        block_size = totals.shape[-1]

        if has_start:
            pltpu.sync_copy(refs[-2], totals)
        else:
            def clear(t, carry):
                totals[t] = jnp.zeros((block_size, block_size), jnp.float32)
                return carry

            lax.fori_loop(0, totals.shape[0], clear, 0)

        for u in range(list_count):
            v = right_pick[u]
            left_list = left_lists[u]
            right_list = right_lists[v]

            def one_term(j, u=u, v=v, left_list=left_list, right_list=right_list):
                i = slots_left[u, j]
                k = slots_right[u, j]
                t = placed(left_ids[u, i] * slab_width + right_ids[v, k], parts)
                term = jnp.dot(left_list[i], right_list[k], preferred_element_type=jnp.float32)
                return t, term

            def add_group(g, carry, one_term=one_term):
                made = [one_term(g * UNROLL + q) for q in range(UNROLL)]
                for t, term in made:
                    totals[t] = totals[t] + term
                return carry

            def add_single(j, carry, one_term=one_term):
                t, term = one_term(j)
                totals[t] = totals[t] + term
                return carry

            count = counts[u]
            groups = count // UNROLL
            lax.fori_loop(0, groups, add_group, 0)
            lax.fori_loop(groups * UNROLL, count, add_single, 0)

    return pair_kernel


def pair_products(slots_left, slots_right, counts, left_ids, right_ids,
                  left_lists, right_lists, right_pick, start=None, targets=None):
    block_size = left_lists[0].shape[-1]
    smem = pl.BlockSpec(memory_space=pltpu.SMEM)
    vmem = pl.BlockSpec(memory_space=pltpu.VMEM)
    operands = [slots_left, slots_right, counts, left_ids, right_ids, *left_lists, *right_lists]
    if start is not None:
        operands.append(start)
        targets = start.shape[0]
    return pl.pallas_call(
        make_pair_kernel(start is not None, right_pick, len(left_lists), len(right_lists)),
        out_shape=jax.ShapeDtypeStruct((targets, block_size, block_size), jnp.float32),
        in_specs=[smem] * 5 + [vmem] * (len(left_lists) + len(right_lists))
        + [pl.BlockSpec(memory_space=pl.ANY)] * (start is not None),
        out_specs=vmem,
        compiler_params=pltpu.CompilerParams(vmem_limit_bytes=60 * 1024 * 1024),
    )(*operands)


def shifted(value, axis, steps):
    count = lax.axis_size(axis)
    pairs = [(source, (source + steps) % count) for source in range(count)]
    return lax.ppermute(value, axis, pairs)


def on_device(left_blocks, left_rows, right_blocks, right_cols, pair_left, pair_right, pair_count):
    block_size = left_blocks.shape[-1]
    left_cap = left_blocks.shape[3]
    right_cap = right_blocks.shape[3]
    piece_count = lax.axis_size("row")
    slab_width = SLAB // piece_count
    targets = ROWS_GROUP * slab_width
    row_here = lax.axis_index("row")
    col_here = lax.axis_index("col")
    own_left = (left_blocks.reshape(left_cap, block_size, block_size), left_rows.reshape(left_cap))
    own_right = (right_blocks.reshape(right_cap, block_size, block_size), right_cols.reshape(right_cap))

    from_below = shifted(own_left, "row", 1)
    from_above = shifted(own_left, "row", -1)
    other_right = shifted(own_right, "col", 1)

    slots_left_all = pair_left.reshape(piece_count, -1)
    slots_right_all = pair_right.reshape(piece_count, -1)
    counts_all = pair_count.reshape(piece_count)

    def pieces_for(offsets):
        piece = (row_here + col_here + jnp.array(offsets, jnp.int32)) % piece_count
        return (jnp.take(slots_left_all, piece, axis=0), jnp.take(slots_right_all, piece, axis=0),
                jnp.take(counts_all, piece, axis=0))

    right_lists = (own_right[0], other_right[0])
    right_id_stack = jnp.stack([own_right[1], other_right[1]])
    sl, sr, cn = pieces_for([0])
    totals = pair_products(sl, sr, cn, own_left[1][None], own_right[1][None],
                           (own_left[0],), (own_right[0],), (0,), targets=targets)
    totals, from_below, from_above = lax.optimization_barrier((totals, from_below, from_above))
    half = left_cap // 2
    far_low = shifted(jax.tree.map(lambda a: a[:half], from_below), "row", 1)
    far_high = shifted(jax.tree.map(lambda a: a[half:], from_above), "row", -1)
    sl, sr, cn = pieces_for([-1, 1, 2])
    far = jax.tree.map(lambda a, b: jnp.concatenate([a, b]), far_low, far_high)
    left_id_stack = jnp.stack([from_below[1], from_above[1], far[1]])
    totals = pair_products(sl, sr, cn, left_id_stack, right_id_stack,
                           (from_below[0], from_above[0], far[0]), right_lists, (1, 1, 0),
                           start=totals)
    width = targets // parts
    owned = jnp.concatenate([
        lax.psum_scatter(totals[part * width:(part + 1) * width], "layer", scatter_dimension=0,
                         tiled=True)
        for part in range(parts)])
    return owned.reshape(1, 1, -1, block_size, block_size)


def solution(mesh):
    in_specs = (
        P("row", "col", "layer", None, None, None),
        P("row", "col", "layer", None),
        P("row", "col", "layer", None, None, None),
        P("row", "col", "layer", None),
        P("row", "col", "layer", None, None),
        P("row", "col", "layer", None, None),
        P("row", "col", "layer", None),
    )
    out_specs = P("col", "row", "layer", None, None)
    return jax.shard_map(
        on_device, mesh=mesh, in_specs=in_specs, out_specs=out_specs, check_vma=False
    )
```

```python
import jax
import jax.numpy as jnp
from jax import lax
from jax.experimental import pallas as pl
from jax.experimental.pallas import tpu as pltpu
from jax.sharding import PartitionSpec as P

SLAB = 128
ROWS_GROUP = 8
UNROLL = 16


def make_pair_kernel(has_start, right_pick, list_count, right_count):
    def pair_kernel(slots_left, slots_right, counts, left_ids, right_ids, *refs):
        left_lists = refs[:list_count]
        right_lists = refs[list_count:list_count + right_count]
        totals = refs[-1]
        slab_width = totals.shape[0] // ROWS_GROUP
        block_size = totals.shape[-1]

        if has_start:
            pltpu.sync_copy(refs[-2], totals)
        else:
            def clear(t, carry):
                totals[t] = jnp.zeros((block_size, block_size), jnp.float32)
                return carry

            lax.fori_loop(0, totals.shape[0], clear, 0)

        for u in range(list_count):
            v = right_pick[u]
            left_list = left_lists[u]
            right_list = right_lists[v]

            def one_term(j, u=u, v=v, left_list=left_list, right_list=right_list):
                i = slots_left[u, j]
                k = slots_right[u, j]
                t = left_ids[u, i] * slab_width + right_ids[v, k]
                term = jnp.dot(left_list[i], right_list[k], preferred_element_type=jnp.float32)
                return t, term

            def add_group(g, carry, one_term=one_term):
                made = [one_term(g * UNROLL + q) for q in range(UNROLL)]
                for t, term in made:
                    totals[t] = totals[t] + term
                return carry

            def add_single(j, carry, one_term=one_term):
                t, term = one_term(j)
                totals[t] = totals[t] + term
                return carry

            count = counts[u]
            groups = count // UNROLL
            lax.fori_loop(0, groups, add_group, 0)
            lax.fori_loop(groups * UNROLL, count, add_single, 0)

    return pair_kernel


def pair_products(slots_left, slots_right, counts, left_ids, right_ids,
                  left_lists, right_lists, right_pick, start=None, targets=None):
    block_size = left_lists[0].shape[-1]
    smem = pl.BlockSpec(memory_space=pltpu.SMEM)
    vmem = pl.BlockSpec(memory_space=pltpu.VMEM)
    operands = [slots_left, slots_right, counts, left_ids, right_ids, *left_lists, *right_lists]
    if start is not None:
        operands.append(start)
        targets = start.shape[0]
    return pl.pallas_call(
        make_pair_kernel(start is not None, right_pick, len(left_lists), len(right_lists)),
        out_shape=jax.ShapeDtypeStruct((targets, block_size, block_size), jnp.float32),
        in_specs=[smem] * 5 + [vmem] * (len(left_lists) + len(right_lists))
        + [pl.BlockSpec(memory_space=pl.ANY)] * (start is not None),
        out_specs=vmem,
        compiler_params=pltpu.CompilerParams(vmem_limit_bytes=60 * 1024 * 1024),
    )(*operands)


def shifted(value, axis, steps):
    count = lax.axis_size(axis)
    pairs = [(source, (source + steps) % count) for source in range(count)]
    return lax.ppermute(value, axis, pairs)


def on_device(left_blocks, left_rows, right_blocks, right_cols, pair_left, pair_right, pair_count):
    block_size = left_blocks.shape[-1]
    left_cap = left_blocks.shape[3]
    right_cap = right_blocks.shape[3]
    piece_count = lax.axis_size("row")
    slab_width = SLAB // piece_count
    targets = ROWS_GROUP * slab_width
    row_here = lax.axis_index("row")
    col_here = lax.axis_index("col")
    own_left = (left_blocks.reshape(left_cap, block_size, block_size), left_rows.reshape(left_cap))
    own_right = (right_blocks.reshape(right_cap, block_size, block_size), right_cols.reshape(right_cap))

    from_below = shifted(own_left, "row", 1)
    from_above = shifted(own_left, "row", -1)
    other_right = shifted(own_right, "col", 1)

    slots_left_all = pair_left.reshape(piece_count, -1)
    slots_right_all = pair_right.reshape(piece_count, -1)
    counts_all = pair_count.reshape(piece_count)

    def pieces_for(offsets):
        piece = (row_here + col_here + jnp.array(offsets, jnp.int32)) % piece_count
        return (jnp.take(slots_left_all, piece, axis=0), jnp.take(slots_right_all, piece, axis=0),
                jnp.take(counts_all, piece, axis=0))

    right_lists = (own_right[0], other_right[0])
    right_id_stack = jnp.stack([own_right[1], other_right[1]])
    sl, sr, cn = pieces_for([0])
    totals = pair_products(sl, sr, cn, own_left[1][None], own_right[1][None],
                           (own_left[0],), (own_right[0],), (0,), targets=targets)
    totals, from_below, from_above = lax.optimization_barrier((totals, from_below, from_above))
    half = left_cap // 2
    far_low = shifted(jax.tree.map(lambda a: a[:half], from_below), "row", 1)
    far_high = shifted(jax.tree.map(lambda a: a[half:], from_above), "row", -1)
    sl, sr, cn = pieces_for([-1, 1, 2])
    far = jax.tree.map(lambda a, b: jnp.concatenate([a, b]), far_low, far_high)
    left_id_stack = jnp.stack([from_below[1], from_above[1], far[1]])
    totals = pair_products(sl, sr, cn, left_id_stack, right_id_stack,
                           (from_below[0], from_above[0], far[0]), right_lists, (1, 1, 0),
                           start=totals)
    owned = lax.psum_scatter(totals, "layer", scatter_dimension=0, tiled=True)
    return owned.reshape(1, 1, -1, block_size, block_size)


def solution(mesh):
    in_specs = (
        P("row", "col", "layer", None, None, None),
        P("row", "col", "layer", None),
        P("row", "col", "layer", None, None, None),
        P("row", "col", "layer", None),
        P("row", "col", "layer", None, None),
        P("row", "col", "layer", None, None),
        P("row", "col", "layer", None),
    )
    out_specs = P("col", "row", "layer", None, None)
    return jax.shard_map(
        on_device, mesh=mesh, in_specs=in_specs, out_specs=out_specs, check_vma=False
    )
```

```python
import jax
import jax.numpy as jnp
from jax import lax
from jax.experimental import pallas as pl
from jax.experimental.pallas import tpu as pltpu
from jax.sharding import PartitionSpec as P

SLAB = 128
ROWS_GROUP = 8
UNROLL = 16


def make_pair_kernel(right_pick, sources):
    list_count = len(right_pick)
    operand_count = sum(len(parts) for parts in sources)

    def pair_kernel(slots_left, slots_right, counts, left_ids, right_ids, *refs):
        operands = refs[:operand_count]
        right_hbm = refs[operand_count:operand_count + 2]
        totals = refs[operand_count + 2]
        left_lists, right_lists, sems = refs[operand_count + 3:]
        slab_width = totals.shape[0] // ROWS_GROUP
        block_size = totals.shape[-1]

        right_copies = [pltpu.make_async_copy(right_hbm[v], right_lists.at[v], sems.at[v])
                        for v in range(2)]
        left_copies = []
        position = 0
        for u, parts in enumerate(sources):
            copies = []
            offset = 0
            for part in parts:
                size = operands[position].shape[0]
                copies.append(pltpu.make_async_copy(
                    operands[position], left_lists.at[u, pl.ds(offset, size)],
                    sems.at[2 + position]))
                offset += size
                position += 1
            left_copies.append(copies)
        started = set()
        for u in range(list_count):
            for copy in left_copies[u]:
                copy.start()
            if right_pick[u] not in started:
                right_copies[right_pick[u]].start()
                started.add(right_pick[u])

        def clear(t, carry):
            totals[t] = jnp.zeros((block_size, block_size), jnp.float32)
            return carry

        lax.fori_loop(0, totals.shape[0], clear, 0)

        waited = set()
        for u in range(list_count):
            v = right_pick[u]
            for copy in left_copies[u]:
                copy.wait()
            if v not in waited:
                right_copies[v].wait()
                waited.add(v)

            def one_term(j, u=u, v=v):
                i = slots_left[u, j]
                k = slots_right[u, j]
                t = left_ids[u, i] * slab_width + right_ids[v, k]
                term = jnp.dot(left_lists[u, i], right_lists[v, k],
                               preferred_element_type=jnp.float32)
                return t, term

            def add_group(g, carry, one_term=one_term):
                made = [one_term(g * UNROLL + q) for q in range(UNROLL)]
                for t, term in made:
                    totals[t] = totals[t] + term
                return carry

            def add_single(j, carry, one_term=one_term):
                t, term = one_term(j)
                totals[t] = totals[t] + term
                return carry

            count = counts[u]
            groups = count // UNROLL
            lax.fori_loop(0, groups, add_group, 0)
            lax.fori_loop(groups * UNROLL, count, add_single, 0)

    return pair_kernel


def pair_products(slots_left, slots_right, counts, left_ids, right_ids,
                  left_sources, right_lists, right_pick, targets):
    block_size = right_lists[0].shape[-1]
    list_cap = right_lists[0].shape[0]
    smem = pl.BlockSpec(memory_space=pltpu.SMEM)
    hbm = pl.BlockSpec(memory_space=pl.ANY)
    flat = [part for parts in left_sources for part in parts]
    return pl.pallas_call(
        make_pair_kernel(right_pick, [tuple(range(len(parts))) for parts in left_sources]),
        out_shape=jax.ShapeDtypeStruct((targets, block_size, block_size), jnp.float32),
        in_specs=[smem] * 5 + [hbm] * (len(flat) + len(right_lists)),
        out_specs=pl.BlockSpec(memory_space=pltpu.VMEM),
        scratch_shapes=[
            pltpu.VMEM((len(left_sources), list_cap, block_size, block_size), jnp.bfloat16),
            pltpu.VMEM((len(right_lists), list_cap, block_size, block_size), jnp.bfloat16),
            pltpu.SemaphoreType.DMA((2 + len(flat),)),
        ],
        compiler_params=pltpu.CompilerParams(vmem_limit_bytes=60 * 1024 * 1024),
    )(slots_left, slots_right, counts, left_ids, right_ids, *flat, *right_lists)


def shifted(value, axis, steps):
    count = lax.axis_size(axis)
    pairs = [(source, (source + steps) % count) for source in range(count)]
    return lax.ppermute(value, axis, pairs)


def on_device(left_blocks, left_rows, right_blocks, right_cols, pair_left, pair_right, pair_count):
    block_size = left_blocks.shape[-1]
    left_cap = left_blocks.shape[3]
    right_cap = right_blocks.shape[3]
    piece_count = lax.axis_size("row")
    slab_width = SLAB // piece_count
    targets = ROWS_GROUP * slab_width
    row_here = lax.axis_index("row")
    col_here = lax.axis_index("col")
    own_left = (left_blocks.reshape(left_cap, block_size, block_size), left_rows.reshape(left_cap))
    own_right = (right_blocks.reshape(right_cap, block_size, block_size), right_cols.reshape(right_cap))

    from_below = shifted(own_left, "row", 1)
    from_above = shifted(own_left, "row", -1)
    other_right = shifted(own_right, "col", 1)

    slots_left_all = pair_left.reshape(piece_count, -1)
    slots_right_all = pair_right.reshape(piece_count, -1)
    counts_all = pair_count.reshape(piece_count)

    def pieces_for(offsets):
        piece = (row_here + col_here + jnp.array(offsets, jnp.int32)) % piece_count
        return (jnp.take(slots_left_all, piece, axis=0), jnp.take(slots_right_all, piece, axis=0),
                jnp.take(counts_all, piece, axis=0))

    half = left_cap // 2
    far_low = shifted(jax.tree.map(lambda a: a[:half], from_below), "row", 1)
    far_high = shifted(jax.tree.map(lambda a: a[half:], from_above), "row", -1)
    far_ids = jnp.concatenate([far_low[1], far_high[1]])
    sl, sr, cn = pieces_for([0, -1, 1, 2])
    left_id_stack = jnp.stack([own_left[1], from_below[1], from_above[1], far_ids])
    right_id_stack = jnp.stack([own_right[1], other_right[1]])
    totals = pair_products(sl, sr, cn, left_id_stack, right_id_stack,
                           ((own_left[0],), (from_below[0],), (from_above[0],),
                            (far_low[0], far_high[0])),
                           (own_right[0], other_right[0]), (0, 1, 1, 0), targets)
    owned = lax.psum_scatter(totals, "layer", scatter_dimension=0, tiled=True)
    return owned.reshape(1, 1, -1, block_size, block_size)


def solution(mesh):
    in_specs = (
        P("row", "col", "layer", None, None, None),
        P("row", "col", "layer", None),
        P("row", "col", "layer", None, None, None),
        P("row", "col", "layer", None),
        P("row", "col", "layer", None, None),
        P("row", "col", "layer", None, None),
        P("row", "col", "layer", None),
    )
    out_specs = P("col", "row", "layer", None, None)
    return jax.shard_map(
        on_device, mesh=mesh, in_specs=in_specs, out_specs=out_specs, check_vma=False
    )
```

```python
import jax
import jax.numpy as jnp
from jax import lax
from jax.experimental import pallas as pl
from jax.experimental.pallas import tpu as pltpu
from jax.sharding import PartitionSpec as P

SLAB = 128
ROWS_GROUP = 8
UNROLL = 16


def make_pair_kernel(right_pick, sources):
    list_count = len(right_pick)
    operand_count = sum(len(parts) for parts in sources)

    def pair_kernel(slots_left, slots_right, counts, left_ids, right_ids, *refs):
        operands = refs[:operand_count]
        right_hbm = refs[operand_count:operand_count + 2]
        totals = refs[operand_count + 2]
        left_lists, right_lists, sems = refs[operand_count + 3:]
        slab_width = totals.shape[0] // ROWS_GROUP
        block_size = totals.shape[-1]

        right_copies = [pltpu.make_async_copy(right_hbm[v], right_lists.at[v], sems.at[v])
                        for v in range(2)]
        left_copies = []
        position = 0
        for u, parts in enumerate(sources):
            copies = []
            offset = 0
            for part in parts:
                size = operands[position].shape[0]
                copies.append(pltpu.make_async_copy(
                    operands[position], left_lists.at[u, pl.ds(offset, size)],
                    sems.at[2 + position]))
                offset += size
                position += 1
            left_copies.append(copies)
        started = set()
        for u in range(list_count):
            for copy in left_copies[u]:
                copy.start()
            if right_pick[u] not in started:
                right_copies[right_pick[u]].start()
                started.add(right_pick[u])

        def clear(t, carry):
            totals[t] = jnp.zeros((block_size, block_size), jnp.float32)
            return carry

        lax.fori_loop(0, totals.shape[0], clear, 0)

        waited = set()
        for u in range(list_count):
            v = right_pick[u]
            for copy in left_copies[u]:
                copy.wait()
            if v not in waited:
                right_copies[v].wait()
                waited.add(v)

            def one_term(j, u=u, v=v):
                i = slots_left[u, j]
                k = slots_right[u, j]
                t = left_ids[u, i] * slab_width + right_ids[v, k]
                term = jnp.dot(left_lists[u, i], right_lists[v, k],
                               preferred_element_type=jnp.float32)
                return t, term

            def add_group(g, carry, one_term=one_term):
                made = [one_term(g * UNROLL + q) for q in range(UNROLL)]
                for t, term in made:
                    totals[t] = totals[t] + term
                return carry

            def add_single(j, carry, one_term=one_term):
                t, term = one_term(j)
                totals[t] = totals[t] + term
                return carry

            count = counts[u]
            groups = count // UNROLL
            lax.fori_loop(0, groups, add_group, 0)
            lax.fori_loop(groups * UNROLL, count, add_single, 0)

    return pair_kernel


def pair_products(slots_left, slots_right, counts, left_ids, right_ids,
                  left_sources, right_lists, right_pick, targets):
    block_size = right_lists[0].shape[-1]
    list_cap = right_lists[0].shape[0]
    smem = pl.BlockSpec(memory_space=pltpu.SMEM)
    hbm = pl.BlockSpec(memory_space=pl.ANY)
    flat = [part for parts in left_sources for part in parts]
    return pl.pallas_call(
        make_pair_kernel(right_pick, [tuple(range(len(parts))) for parts in left_sources]),
        out_shape=jax.ShapeDtypeStruct((targets, block_size, block_size), jnp.float32),
        in_specs=[smem] * 5 + [hbm] * (len(flat) + len(right_lists)),
        out_specs=pl.BlockSpec(memory_space=pltpu.VMEM),
        scratch_shapes=[
            pltpu.VMEM((len(left_sources), list_cap, block_size, block_size), jnp.bfloat16),
            pltpu.VMEM((len(right_lists), list_cap, block_size, block_size), jnp.bfloat16),
            pltpu.SemaphoreType.DMA((2 + len(flat),)),
        ],
        compiler_params=pltpu.CompilerParams(vmem_limit_bytes=60 * 1024 * 1024),
    )(slots_left, slots_right, counts, left_ids, right_ids, *flat, *right_lists)


def shifted(value, axis, steps):
    count = lax.axis_size(axis)
    pairs = [(source, (source + steps) % count) for source in range(count)]
    return lax.ppermute(value, axis, pairs)


def on_device(left_blocks, left_rows, right_blocks, right_cols, pair_left, pair_right, pair_count):
    block_size = left_blocks.shape[-1]
    left_cap = left_blocks.shape[3]
    right_cap = right_blocks.shape[3]
    piece_count = lax.axis_size("row")
    slab_width = SLAB // piece_count
    targets = ROWS_GROUP * slab_width
    row_here = lax.axis_index("row")
    col_here = lax.axis_index("col")
    own_left = (left_blocks.reshape(left_cap, block_size, block_size), left_rows.reshape(left_cap))
    own_right = (right_blocks.reshape(right_cap, block_size, block_size), right_cols.reshape(right_cap))

    left_ids_all = lax.all_gather(own_left[1], "row")
    from_below = shifted(own_left[0], "row", 1)
    from_above = shifted(own_left[0], "row", -1)
    other_right = shifted(own_right, "col", 1)

    slots_left_all = pair_left.reshape(piece_count, -1)
    slots_right_all = pair_right.reshape(piece_count, -1)
    counts_all = pair_count.reshape(piece_count)

    def pieces_for(offsets):
        piece = (row_here + col_here + jnp.array(offsets, jnp.int32)) % piece_count
        return (jnp.take(slots_left_all, piece, axis=0), jnp.take(slots_right_all, piece, axis=0),
                jnp.take(counts_all, piece, axis=0))

    half = left_cap // 2
    far_low = shifted(from_below[:half], "row", 1)
    far_high = shifted(from_above[half:], "row", -1)
    sl, sr, cn = pieces_for([0, -1, 1, 2])
    offsets = jnp.array([0, -1, 1, 2], jnp.int32)
    left_id_stack = jnp.take(left_ids_all, (row_here + offsets) % piece_count, axis=0)
    right_id_stack = jnp.stack([own_right[1], other_right[1]])
    totals = pair_products(sl, sr, cn, left_id_stack, right_id_stack,
                           ((own_left[0],), (from_below,), (from_above,), (far_low, far_high)),
                           (own_right[0], other_right[0]), (0, 1, 1, 0), targets)
    owned = lax.psum_scatter(totals, "layer", scatter_dimension=0, tiled=True)
    return owned.reshape(1, 1, -1, block_size, block_size)


def solution(mesh):
    in_specs = (
        P("row", "col", "layer", None, None, None),
        P("row", "col", "layer", None),
        P("row", "col", "layer", None, None, None),
        P("row", "col", "layer", None),
        P("row", "col", "layer", None, None),
        P("row", "col", "layer", None, None),
        P("row", "col", "layer", None),
    )
    out_specs = P("col", "row", "layer", None, None)
    return jax.shard_map(
        on_device, mesh=mesh, in_specs=in_specs, out_specs=out_specs, check_vma=False
    )
```

```python
import jax
import jax.numpy as jnp
from jax import lax
from jax.experimental import pallas as pl
from jax.experimental.pallas import tpu as pltpu
from jax.sharding import Mesh, PartitionSpec as P

SLAB = 128
ROWS_GROUP = 8
UNROLL = 16


def pair_kernel(slots_left, slots_right, counts, left_ids, right_ids, pick,
                own_left, from_below, from_above, left_pair, own_right, right_pair,
                totals, left_lists, right_lists, sems):
    slab_width = totals.shape[0] // ROWS_GROUP
    block_size = totals.shape[-1]
    copies = [
        [pltpu.make_async_copy(own_left, left_lists.at[0], sems.at[0]),
         pltpu.make_async_copy(own_right, right_lists.at[0], sems.at[1])],
        [pltpu.make_async_copy(from_below, left_lists.at[1], sems.at[2]),
         pltpu.make_async_copy(right_pair.at[pick[0]], right_lists.at[1], sems.at[3])],
        [pltpu.make_async_copy(from_above, left_lists.at[2], sems.at[4])],
        [pltpu.make_async_copy(left_pair.at[pick[1]], left_lists.at[3], sems.at[5])],
    ]
    for group in copies:
        for copy in group:
            copy.start()

    def clear(t, carry):
        totals[t] = jnp.zeros((block_size, block_size), jnp.float32)
        return carry

    lax.fori_loop(0, totals.shape[0], clear, 0)

    for u, v in enumerate((0, 1, 1, 0)):
        for copy in copies[u]:
            copy.wait()

        def one_term(j, u=u, v=v):
            i = slots_left[u, j]
            k = slots_right[u, j]
            t = left_ids[u, i] * slab_width + right_ids[v, k]
            term = jnp.dot(left_lists[u, i], right_lists[v, k], preferred_element_type=jnp.float32)
            return t, term

        def add_group(g, carry, one_term=one_term):
            made = [one_term(g * UNROLL + q) for q in range(UNROLL)]
            for t, term in made:
                totals[t] = totals[t] + term
            return carry

        def add_single(j, carry, one_term=one_term):
            t, term = one_term(j)
            totals[t] = totals[t] + term
            return carry

        count = counts[u]
        groups = count // UNROLL
        lax.fori_loop(0, groups, add_group, 0)
        lax.fori_loop(groups * UNROLL, count, add_single, 0)


def pair_products(scalars, lists, targets):
    own_left = lists[0]
    list_cap, block_size = own_left.shape[0], own_left.shape[-1]
    smem = pl.BlockSpec(memory_space=pltpu.SMEM)
    hbm = pl.BlockSpec(memory_space=pl.ANY)
    return pl.pallas_call(
        pair_kernel,
        out_shape=jax.ShapeDtypeStruct((targets, block_size, block_size), jnp.float32),
        in_specs=[smem] * len(scalars) + [hbm] * len(lists),
        out_specs=pl.BlockSpec(memory_space=pltpu.VMEM),
        scratch_shapes=[
            pltpu.VMEM((4, list_cap, block_size, block_size), jnp.bfloat16),
            pltpu.VMEM((2, list_cap, block_size, block_size), jnp.bfloat16),
            pltpu.SemaphoreType.DMA((6,)),
        ],
        compiler_params=pltpu.CompilerParams(vmem_limit_bytes=60 * 1024 * 1024),
    )(*scalars, *lists)


def shifted(value, axis, steps):
    count = lax.axis_size(axis)
    pairs = [(source, (source + steps) % count) for source in range(count)]
    return lax.ppermute(value, axis, pairs)


ROW = ("row_high", "row_low")
LAYER = ("layer_high", "layer_low")


def on_device(left_blocks, left_rows, right_blocks, right_cols, pair_left, pair_right, pair_count):
    block_size = left_blocks.shape[-1]
    left_cap = left_blocks.shape[3]
    right_cap = right_blocks.shape[3]
    low_count = lax.axis_size("row_low")
    piece_count = lax.axis_size("row_high") * low_count
    slab_width = SLAB // piece_count
    targets = ROWS_GROUP * slab_width
    row_high = lax.axis_index("row_high")
    row_here = row_high * low_count + lax.axis_index("row_low")
    col_here = lax.axis_index("col")
    own_left = left_blocks.reshape(left_cap, block_size, block_size)
    own_right = right_blocks.reshape(right_cap, block_size, block_size)

    from_below = shifted(own_left, ROW, 1)
    from_above = shifted(own_left, ROW, -1)
    left_pair = lax.all_gather(own_left, "row_high")
    right_pair = lax.all_gather(own_right, "col")
    left_ids_all = lax.all_gather(left_rows.reshape(left_cap), ROW)
    right_ids_pair = lax.all_gather(right_cols.reshape(right_cap), "col")

    slots_left_all = pair_left.reshape(piece_count, -1)
    slots_right_all = pair_right.reshape(piece_count, -1)
    counts_all = pair_count.reshape(piece_count)
    offsets = jnp.array([0, -1, 1, 2], jnp.int32)
    piece = (row_here + col_here + offsets) % piece_count
    left_id_stack = jnp.take(left_ids_all, (row_here + offsets) % piece_count, axis=0)
    right_id_stack = jnp.take(right_ids_pair, jnp.stack([col_here, 1 - col_here]), axis=0)
    pick = jnp.stack([1 - col_here, 1 - row_high]).astype(jnp.int32)
    scalars = (jnp.take(slots_left_all, piece, axis=0), jnp.take(slots_right_all, piece, axis=0),
               jnp.take(counts_all, piece, axis=0), left_id_stack, right_id_stack, pick)
    totals = pair_products(scalars, (own_left, from_below, from_above, left_pair, own_right,
                                     right_pair), targets)
    owned = lax.psum_scatter(totals, LAYER, scatter_dimension=0, tiled=True)
    return owned.reshape(1, 1, -1, block_size, block_size)


def solution(mesh):
    devices = mesh.devices
    rows, cols, layers = devices.shape
    split = Mesh(devices.reshape(2, rows // 2, cols, 4, layers // 4),
                 ROW + ("col",) + LAYER)
    in_specs = (
        P(ROW, "col", LAYER, None, None, None),
        P(ROW, "col", LAYER, None),
        P(ROW, "col", LAYER, None, None, None),
        P(ROW, "col", LAYER, None),
        P(ROW, "col", LAYER, None, None),
        P(ROW, "col", LAYER, None, None),
        P(ROW, "col", LAYER, None),
    )
    out_specs = P("col", ROW, LAYER, None, None)
    return jax.shard_map(
        on_device, mesh=split, in_specs=in_specs, out_specs=out_specs, check_vma=False
    )
```

```python
import jax
import jax.numpy as jnp
from jax import lax
from jax.experimental import pallas as pl
from jax.experimental.pallas import tpu as pltpu
from jax.sharding import PartitionSpec as P

SLAB = 128
ROWS_GROUP = 8
UNROLL = 16


def pair_kernel(slots_left, slots_right, counts, left_ids, right_ids, pick,
                own_left, from_below, from_above, far_low, far_high, own_right, right_pair,
                totals, left_lists, right_lists, sems):
    half = far_low.shape[0]
    slab_width = totals.shape[0] // ROWS_GROUP
    block_size = totals.shape[-1]
    copies = [
        [pltpu.make_async_copy(own_left, left_lists.at[0], sems.at[0]),
         pltpu.make_async_copy(own_right, right_lists.at[0], sems.at[1])],
        [pltpu.make_async_copy(from_below, left_lists.at[1], sems.at[2]),
         pltpu.make_async_copy(right_pair.at[pick[0]], right_lists.at[1], sems.at[3])],
        [pltpu.make_async_copy(from_above, left_lists.at[2], sems.at[4])],
        [pltpu.make_async_copy(far_low, left_lists.at[3, pl.ds(0, half)], sems.at[5]),
         pltpu.make_async_copy(far_high, left_lists.at[3, pl.ds(half, half)], sems.at[6])],
    ]
    for group in copies:
        for copy in group:
            copy.start()

    def clear(t, carry):
        totals[t] = jnp.zeros((block_size, block_size), jnp.float32)
        return carry

    lax.fori_loop(0, totals.shape[0], clear, 0)

    for u, v in enumerate((0, 1, 1, 0)):
        for copy in copies[u]:
            copy.wait()

        def one_term(j, u=u, v=v):
            i = slots_left[u, j]
            k = slots_right[u, j]
            t = left_ids[u, i] * slab_width + right_ids[v, k]
            term = jnp.dot(left_lists[u, i], right_lists[v, k], preferred_element_type=jnp.float32)
            return t, term

        def add_group(g, carry, one_term=one_term):
            made = [one_term(g * UNROLL + q) for q in range(UNROLL)]
            for t, term in made:
                totals[t] = totals[t] + term
            return carry

        def add_single(j, carry, one_term=one_term):
            t, term = one_term(j)
            totals[t] = totals[t] + term
            return carry

        count = counts[u]
        groups = count // UNROLL
        lax.fori_loop(0, groups, add_group, 0)
        lax.fori_loop(groups * UNROLL, count, add_single, 0)


def pair_products(scalars, lists, targets):
    own_left = lists[0]
    list_cap, block_size = own_left.shape[0], own_left.shape[-1]
    smem = pl.BlockSpec(memory_space=pltpu.SMEM)
    hbm = pl.BlockSpec(memory_space=pl.ANY)
    return pl.pallas_call(
        pair_kernel,
        out_shape=jax.ShapeDtypeStruct((targets, block_size, block_size), jnp.float32),
        in_specs=[smem] * len(scalars) + [hbm] * len(lists),
        out_specs=pl.BlockSpec(memory_space=pltpu.VMEM),
        scratch_shapes=[
            pltpu.VMEM((4, list_cap, block_size, block_size), jnp.bfloat16),
            pltpu.VMEM((2, list_cap, block_size, block_size), jnp.bfloat16),
            pltpu.SemaphoreType.DMA((7,)),
        ],
        compiler_params=pltpu.CompilerParams(vmem_limit_bytes=60 * 1024 * 1024),
    )(*scalars, *lists)


def shifted(value, axis, steps):
    count = lax.axis_size(axis)
    pairs = [(source, (source + steps) % count) for source in range(count)]
    return lax.ppermute(value, axis, pairs)


def on_device(left_blocks, left_rows, right_blocks, right_cols, pair_left, pair_right, pair_count):
    block_size = left_blocks.shape[-1]
    left_cap = left_blocks.shape[3]
    right_cap = right_blocks.shape[3]
    piece_count = lax.axis_size("row")
    slab_width = SLAB // piece_count
    targets = ROWS_GROUP * slab_width
    row_here = lax.axis_index("row")
    col_here = lax.axis_index("col")
    own_left = left_blocks.reshape(left_cap, block_size, block_size)
    own_right = right_blocks.reshape(right_cap, block_size, block_size)
    own_ids = left_rows.reshape(left_cap)

    ids_below = shifted(own_ids, "row", 1)
    ids_above = shifted(own_ids, "row", -1)
    ids_far = shifted(own_ids, "row", 2)
    from_below = shifted(own_left, "row", 1)
    from_above = shifted(own_left, "row", -1)
    right_pair = lax.all_gather(own_right, "col")
    right_ids_pair = lax.all_gather(right_cols.reshape(right_cap), "col")
    half = left_cap // 2
    far_low = shifted(from_below[:half], "row", 1)
    far_high = shifted(from_above[half:], "row", -1)

    slots_left_all = pair_left.reshape(piece_count, -1)
    slots_right_all = pair_right.reshape(piece_count, -1)
    counts_all = pair_count.reshape(piece_count)
    offsets = jnp.array([0, -1, 1, 2], jnp.int32)
    piece = (row_here + col_here + offsets) % piece_count
    left_id_stack = jnp.stack([own_ids, ids_below, ids_above, ids_far])
    right_id_stack = jnp.take(right_ids_pair, jnp.stack([col_here, 1 - col_here]), axis=0)
    pick = jnp.stack([1 - col_here, col_here]).astype(jnp.int32)
    scalars = (jnp.take(slots_left_all, piece, axis=0), jnp.take(slots_right_all, piece, axis=0),
               jnp.take(counts_all, piece, axis=0), left_id_stack, right_id_stack, pick)
    totals = pair_products(scalars, (own_left, from_below, from_above, far_low, far_high,
                                     own_right, right_pair), targets)
    owned = lax.psum_scatter(totals, "layer", scatter_dimension=0, tiled=True)
    return owned.reshape(1, 1, -1, block_size, block_size)


def solution(mesh):
    in_specs = (
        P("row", "col", "layer", None, None, None),
        P("row", "col", "layer", None),
        P("row", "col", "layer", None, None, None),
        P("row", "col", "layer", None),
        P("row", "col", "layer", None, None),
        P("row", "col", "layer", None, None),
        P("row", "col", "layer", None),
    )
    out_specs = P("col", "row", "layer", None, None)
    return jax.shard_map(
        on_device, mesh=mesh, in_specs=in_specs, out_specs=out_specs, check_vma=False
    )
```

```python
import jax
import jax.numpy as jnp
from jax import lax
from jax.experimental import pallas as pl
from jax.experimental.pallas import tpu as pltpu
from jax.sharding import PartitionSpec as P

SLAB = 128
ROWS_GROUP = 8
UNROLL = 16


def pair_kernel(slots_left, slots_right, counts, left_ids, right_ids, pick,
                own_left, below_low, below_high, above_low, above_high, far_low, far_high,
                own_right, right_pair, totals, left_lists, right_lists, sems):
    half = far_low.shape[0]
    slab_width = totals.shape[0] // ROWS_GROUP
    block_size = totals.shape[-1]
    copies = [
        [pltpu.make_async_copy(own_left, left_lists.at[0], sems.at[0]),
         pltpu.make_async_copy(own_right, right_lists.at[0], sems.at[1])],
        [pltpu.make_async_copy(below_low, left_lists.at[1, pl.ds(0, half)], sems.at[2]),
         pltpu.make_async_copy(below_high, left_lists.at[1, pl.ds(half, half)], sems.at[7]),
         pltpu.make_async_copy(right_pair.at[pick[0]], right_lists.at[1], sems.at[3])],
        [pltpu.make_async_copy(above_low, left_lists.at[2, pl.ds(0, half)], sems.at[4]),
         pltpu.make_async_copy(above_high, left_lists.at[2, pl.ds(half, half)], sems.at[8])],
        [pltpu.make_async_copy(far_low, left_lists.at[3, pl.ds(0, half)], sems.at[5]),
         pltpu.make_async_copy(far_high, left_lists.at[3, pl.ds(half, half)], sems.at[6])],
    ]
    for group in copies:
        for copy in group:
            copy.start()

    def clear(t, carry):
        totals[t] = jnp.zeros((block_size, block_size), jnp.float32)
        return carry

    lax.fori_loop(0, totals.shape[0], clear, 0)

    for u, v in enumerate((0, 1, 1, 0)):
        for copy in copies[u]:
            copy.wait()

        def one_term(j, u=u, v=v):
            i = slots_left[u, j]
            k = slots_right[u, j]
            t = left_ids[u, i] * slab_width + right_ids[v, k]
            term = jnp.dot(left_lists[u, i], right_lists[v, k], preferred_element_type=jnp.float32)
            return t, term

        def add_group(g, carry, one_term=one_term):
            made = [one_term(g * UNROLL + q) for q in range(UNROLL)]
            for t, term in made:
                totals[t] = totals[t] + term
            return carry

        def add_single(j, carry, one_term=one_term):
            t, term = one_term(j)
            totals[t] = totals[t] + term
            return carry

        count = counts[u]
        groups = count // UNROLL
        lax.fori_loop(0, groups, add_group, 0)
        lax.fori_loop(groups * UNROLL, count, add_single, 0)


def pair_products(scalars, lists, targets):
    own_left = lists[0]
    list_cap, block_size = own_left.shape[0], own_left.shape[-1]
    smem = pl.BlockSpec(memory_space=pltpu.SMEM)
    hbm = pl.BlockSpec(memory_space=pl.ANY)
    return pl.pallas_call(
        pair_kernel,
        out_shape=jax.ShapeDtypeStruct((targets, block_size, block_size), jnp.float32),
        in_specs=[smem] * len(scalars) + [hbm] * len(lists),
        out_specs=pl.BlockSpec(memory_space=pltpu.VMEM),
        scratch_shapes=[
            pltpu.VMEM((4, list_cap, block_size, block_size), jnp.bfloat16),
            pltpu.VMEM((2, list_cap, block_size, block_size), jnp.bfloat16),
            pltpu.SemaphoreType.DMA((9,)),
        ],
        compiler_params=pltpu.CompilerParams(vmem_limit_bytes=60 * 1024 * 1024),
    )(*scalars, *lists)


def shifted(value, axis, steps):
    count = lax.axis_size(axis)
    pairs = [(source, (source + steps) % count) for source in range(count)]
    return lax.ppermute(value, axis, pairs)


def on_device(left_blocks, left_rows, right_blocks, right_cols, pair_left, pair_right, pair_count):
    block_size = left_blocks.shape[-1]
    left_cap = left_blocks.shape[3]
    right_cap = right_blocks.shape[3]
    piece_count = lax.axis_size("row")
    slab_width = SLAB // piece_count
    targets = ROWS_GROUP * slab_width
    row_here = lax.axis_index("row")
    col_here = lax.axis_index("col")
    own_left = left_blocks.reshape(left_cap, block_size, block_size)
    own_right = right_blocks.reshape(right_cap, block_size, block_size)
    own_ids = left_rows.reshape(left_cap)

    ids_below = shifted(own_ids, "row", 1)
    ids_above = shifted(own_ids, "row", -1)
    ids_far = shifted(own_ids, "row", 2)
    half = left_cap // 2
    own_low, own_high = own_left[:half], own_left[half:]
    below_low = shifted(own_low, "row", 1)
    above_high = shifted(own_high, "row", -1)
    right_pair = lax.all_gather(own_right, "col")
    right_ids_pair = lax.all_gather(right_cols.reshape(right_cap), "col")
    below_low, above_high, own_low, own_high, ids_below, ids_above, ids_far = (
        lax.optimization_barrier(
            (below_low, above_high, own_low, own_high, ids_below, ids_above, ids_far)))
    below_high = shifted(own_high, "row", 1)
    above_low = shifted(own_low, "row", -1)
    far_low = shifted(below_low, "row", 1)
    far_high = shifted(above_high, "row", -1)

    slots_left_all = pair_left.reshape(piece_count, -1)
    slots_right_all = pair_right.reshape(piece_count, -1)
    counts_all = pair_count.reshape(piece_count)
    offsets = jnp.array([0, -1, 1, 2], jnp.int32)
    piece = (row_here + col_here + offsets) % piece_count
    left_id_stack = jnp.stack([own_ids, ids_below, ids_above, ids_far])
    right_id_stack = jnp.take(right_ids_pair, jnp.stack([col_here, 1 - col_here]), axis=0)
    pick = jnp.stack([1 - col_here, col_here]).astype(jnp.int32)
    scalars = (jnp.take(slots_left_all, piece, axis=0), jnp.take(slots_right_all, piece, axis=0),
               jnp.take(counts_all, piece, axis=0), left_id_stack, right_id_stack, pick)
    totals = pair_products(scalars, (own_left, below_low, below_high, above_low, above_high,
                                     far_low, far_high, own_right, right_pair), targets)
    owned = lax.psum_scatter(totals, "layer", scatter_dimension=0, tiled=True)
    return owned.reshape(1, 1, -1, block_size, block_size)


def solution(mesh):
    in_specs = (
        P("row", "col", "layer", None, None, None),
        P("row", "col", "layer", None),
        P("row", "col", "layer", None, None, None),
        P("row", "col", "layer", None),
        P("row", "col", "layer", None, None),
        P("row", "col", "layer", None, None),
        P("row", "col", "layer", None),
    )
    out_specs = P("col", "row", "layer", None, None)
    return jax.shard_map(
        on_device, mesh=mesh, in_specs=in_specs, out_specs=out_specs, check_vma=False
    )
```

```python
import jax
import jax.numpy as jnp
from jax import lax
from jax.experimental import pallas as pl
from jax.experimental.pallas import tpu as pltpu
from jax.sharding import PartitionSpec as P

SLAB = 128
ROWS_GROUP = 8
UNROLL = 16


def make_pair_kernel(parts, right_of, right_count, has_start):
    left_count = sum(parts)

    def pair_kernel(slots_left, slots_right, counts, left_ids, right_ids, pick, *refs):
        left_refs = refs[:left_count]
        right_refs = refs[left_count:left_count + right_count]
        start = refs[left_count + right_count] if has_start else None
        totals, left_lists, right_lists, sems = refs[-4:]
        slab_width = totals.shape[0] // ROWS_GROUP
        block_size = totals.shape[-1]
        copies = []
        position = 0
        for u, count in enumerate(parts):
            offset = 0
            group = []
            for _ in range(count):
                size = left_refs[position].shape[0]
                group.append(pltpu.make_async_copy(
                    left_refs[position], left_lists.at[u, pl.ds(offset, size)], sems.at[position]))
                offset += size
                position += 1
            copies.append(group)
        right_copies = [pltpu.make_async_copy(right_refs[0], right_lists.at[0], sems.at[left_count])]
        if right_count > 1:
            right_copies.append(pltpu.make_async_copy(
                right_refs[1].at[pick[0]], right_lists.at[1], sems.at[left_count + 1]))
        if has_start:
            start_copy = pltpu.make_async_copy(start, totals, sems.at[left_count + right_count])
            start_copy.start()
        for u, group in enumerate(copies):
            for copy in group:
                copy.start()
            if u == 0:
                for copy in right_copies:
                    copy.start()

        if has_start:
            start_copy.wait()
        else:
            def clear(t, carry):
                totals[t] = jnp.zeros((block_size, block_size), jnp.float32)
                return carry

            lax.fori_loop(0, totals.shape[0], clear, 0)

        for u, group in enumerate(copies):
            v = right_of[u]
            for copy in group:
                copy.wait()
            if u == 0:
                for copy in right_copies:
                    copy.wait()

            def one_term(j, u=u, v=v):
                i = slots_left[u, j]
                k = slots_right[u, j]
                t = left_ids[u, i] * slab_width + right_ids[v, k]
                term = jnp.dot(left_lists[u, i], right_lists[v, k],
                               preferred_element_type=jnp.float32)
                return t, term

            def add_group(g, carry, one_term=one_term):
                made = [one_term(g * UNROLL + q) for q in range(UNROLL)]
                for t, term in made:
                    totals[t] = totals[t] + term
                return carry

            def add_single(j, carry, one_term=one_term):
                t, term = one_term(j)
                totals[t] = totals[t] + term
                return carry

            count = counts[u]
            groups = count // UNROLL
            lax.fori_loop(0, groups, add_group, 0)
            lax.fori_loop(groups * UNROLL, count, add_single, 0)

    return pair_kernel


def pair_products(scalars, left_parts, right_lists, right_of, targets, start=None):
    own_left = left_parts[0][0]
    list_cap, block_size = own_left.shape[0] * len(left_parts[0]), own_left.shape[-1]
    smem = pl.BlockSpec(memory_space=pltpu.SMEM)
    hbm = pl.BlockSpec(memory_space=pl.ANY)
    flat = [part for parts in left_parts for part in parts]
    extra = [] if start is None else [start]
    operands = flat + list(right_lists) + extra
    return pl.pallas_call(
        make_pair_kernel([len(parts) for parts in left_parts], right_of, len(right_lists),
                         start is not None),
        out_shape=jax.ShapeDtypeStruct((targets, block_size, block_size), jnp.float32),
        in_specs=[smem] * len(scalars) + [hbm] * len(operands),
        out_specs=pl.BlockSpec(memory_space=pltpu.VMEM),
        scratch_shapes=[
            pltpu.VMEM((len(left_parts), list_cap, block_size, block_size), jnp.bfloat16),
            pltpu.VMEM((2, list_cap, block_size, block_size), jnp.bfloat16),
            pltpu.SemaphoreType.DMA((len(operands),)),
        ],
        compiler_params=pltpu.CompilerParams(vmem_limit_bytes=60 * 1024 * 1024),
    )(*scalars, *operands)


def shifted(value, axis, steps):
    count = lax.axis_size(axis)
    pairs = [(source, (source + steps) % count) for source in range(count)]
    return lax.ppermute(value, axis, pairs)


def on_device(left_blocks, left_rows, right_blocks, right_cols, pair_left, pair_right, pair_count):
    block_size = left_blocks.shape[-1]
    left_cap = left_blocks.shape[3]
    right_cap = right_blocks.shape[3]
    piece_count = lax.axis_size("row")
    slab_width = SLAB // piece_count
    targets = ROWS_GROUP * slab_width
    row_here = lax.axis_index("row")
    col_here = lax.axis_index("col")
    own_left = left_blocks.reshape(left_cap, block_size, block_size)
    own_right = right_blocks.reshape(right_cap, block_size, block_size)
    own_ids = left_rows.reshape(left_cap)

    ids_below = shifted(own_ids, "row", 1)
    ids_above = shifted(own_ids, "row", -1)
    ids_far = shifted(own_ids, "row", 2)
    half = left_cap // 2
    own_low, own_high = own_left[:half], own_left[half:]
    below_low = shifted(own_low, "row", 1)
    above_high = shifted(own_high, "row", -1)
    right_pair = lax.all_gather(own_right, "col")
    right_ids_pair = lax.all_gather(right_cols.reshape(right_cap), "col")
    below_low, above_high, own_low, own_high, ids_below, ids_above, ids_far = (
        lax.optimization_barrier(
            (below_low, above_high, own_low, own_high, ids_below, ids_above, ids_far)))
    below_high = shifted(own_high, "row", 1)
    above_low = shifted(own_low, "row", -1)
    far_low = shifted(below_low, "row", 1)
    far_high = shifted(above_high, "row", -1)

    slots_left_all = pair_left.reshape(piece_count, -1)
    slots_right_all = pair_right.reshape(piece_count, -1)
    counts_all = pair_count.reshape(piece_count)
    right_id_stack = jnp.take(right_ids_pair, jnp.stack([col_here, 1 - col_here]), axis=0)
    pick = jnp.stack([1 - col_here, col_here]).astype(jnp.int32)

    def scalars_for(offsets, id_lists):
        piece = (row_here + col_here + jnp.array(offsets, jnp.int32)) % piece_count
        return (jnp.take(slots_left_all, piece, axis=0), jnp.take(slots_right_all, piece, axis=0),
                jnp.take(counts_all, piece, axis=0), jnp.stack(id_lists), right_id_stack, pick)

    totals = pair_products(scalars_for([0, -1, 1], [own_ids, ids_below, ids_above]),
                           ((own_left,), (below_low, below_high), (above_low, above_high)),
                           (own_right, right_pair), (0, 1, 1), targets)
    totals = pair_products(scalars_for([2], [ids_far]), ((far_low, far_high),),
                           (own_right,), (0,), targets, start=totals)
    owned = lax.psum_scatter(totals, "layer", scatter_dimension=0, tiled=True)
    return owned.reshape(1, 1, -1, block_size, block_size)


def solution(mesh):
    in_specs = (
        P("row", "col", "layer", None, None, None),
        P("row", "col", "layer", None),
        P("row", "col", "layer", None, None, None),
        P("row", "col", "layer", None),
        P("row", "col", "layer", None, None),
        P("row", "col", "layer", None, None),
        P("row", "col", "layer", None),
    )
    out_specs = P("col", "row", "layer", None, None)
    return jax.shard_map(
        on_device, mesh=mesh, in_specs=in_specs, out_specs=out_specs, check_vma=False
    )
```

```python
import jax
import jax.numpy as jnp
from jax import lax
from jax.experimental import pallas as pl
from jax.experimental.pallas import tpu as pltpu
from jax.sharding import PartitionSpec as P

SLAB = 128
ROWS_GROUP = 8
UNROLL = 16


def pair_kernel(slots_left, slots_right, counts, places, pick,
                own_left, below_low, below_high, above_low, above_high, far_low, far_high,
                own_right, right_pair, totals, left_lists, right_lists, sems):
    half = far_low.shape[0]
    block_size = totals.shape[-1]
    copies = [
        [pltpu.make_async_copy(own_left, left_lists.at[0], sems.at[0]),
         pltpu.make_async_copy(own_right, right_lists.at[0], sems.at[1])],
        [pltpu.make_async_copy(below_low, left_lists.at[1, pl.ds(0, half)], sems.at[2]),
         pltpu.make_async_copy(below_high, left_lists.at[1, pl.ds(half, half)], sems.at[7]),
         pltpu.make_async_copy(right_pair.at[pick[0]], right_lists.at[1], sems.at[3])],
        [pltpu.make_async_copy(above_low, left_lists.at[2, pl.ds(0, half)], sems.at[4]),
         pltpu.make_async_copy(above_high, left_lists.at[2, pl.ds(half, half)], sems.at[8])],
        [pltpu.make_async_copy(far_low, left_lists.at[3, pl.ds(0, half)], sems.at[5]),
         pltpu.make_async_copy(far_high, left_lists.at[3, pl.ds(half, half)], sems.at[6])],
    ]
    for group in copies:
        for copy in group:
            copy.start()

    def clear(t, carry):
        totals[t] = jnp.zeros((block_size, block_size), jnp.float32)
        return carry

    lax.fori_loop(0, totals.shape[0], clear, 0)

    for u, v in enumerate((0, 1, 1, 0)):
        for copy in copies[u]:
            copy.wait()

        def one_term(j, u=u, v=v):
            i = slots_left[u, j]
            k = slots_right[u, j]
            t = places[u, j]
            term = jnp.dot(left_lists[u, i], right_lists[v, k], preferred_element_type=jnp.float32)
            return t, term

        def add_group(g, carry, one_term=one_term):
            made = [one_term(g * UNROLL + q) for q in range(UNROLL)]
            for t, term in made:
                totals[t] = totals[t] + term
            return carry

        def add_single(j, carry, one_term=one_term):
            t, term = one_term(j)
            totals[t] = totals[t] + term
            return carry

        count = counts[u]
        groups = count // UNROLL
        lax.fori_loop(0, groups, add_group, 0)
        lax.fori_loop(groups * UNROLL, count, add_single, 0)


def pair_products(scalars, lists, targets):
    own_left = lists[0]
    list_cap, block_size = own_left.shape[0], own_left.shape[-1]
    smem = pl.BlockSpec(memory_space=pltpu.SMEM)
    hbm = pl.BlockSpec(memory_space=pl.ANY)
    return pl.pallas_call(
        pair_kernel,
        out_shape=jax.ShapeDtypeStruct((targets, block_size, block_size), jnp.float32),
        in_specs=[smem] * len(scalars) + [hbm] * len(lists),
        out_specs=pl.BlockSpec(memory_space=pltpu.VMEM),
        scratch_shapes=[
            pltpu.VMEM((4, list_cap, block_size, block_size), jnp.bfloat16),
            pltpu.VMEM((2, list_cap, block_size, block_size), jnp.bfloat16),
            pltpu.SemaphoreType.DMA((9,)),
        ],
        compiler_params=pltpu.CompilerParams(vmem_limit_bytes=60 * 1024 * 1024),
    )(*scalars, *lists)


def shifted(value, axis, steps):
    count = lax.axis_size(axis)
    pairs = [(source, (source + steps) % count) for source in range(count)]
    return lax.ppermute(value, axis, pairs)


def on_device(left_blocks, left_rows, right_blocks, right_cols, pair_left, pair_right, pair_count):
    block_size = left_blocks.shape[-1]
    left_cap = left_blocks.shape[3]
    right_cap = right_blocks.shape[3]
    piece_count = lax.axis_size("row")
    slab_width = SLAB // piece_count
    targets = ROWS_GROUP * slab_width
    row_here = lax.axis_index("row")
    col_here = lax.axis_index("col")
    own_left = left_blocks.reshape(left_cap, block_size, block_size)
    own_right = right_blocks.reshape(right_cap, block_size, block_size)
    own_ids = left_rows.reshape(left_cap)

    ids_below = shifted(own_ids, "row", 1)
    ids_above = shifted(own_ids, "row", -1)
    ids_far = shifted(own_ids, "row", 2)
    half = left_cap // 2
    own_low, own_high = own_left[:half], own_left[half:]
    below_low = shifted(own_low, "row", 1)
    above_high = shifted(own_high, "row", -1)
    right_pair = lax.all_gather(own_right, "col")
    right_ids_pair = lax.all_gather(right_cols.reshape(right_cap), "col")
    below_low, above_high, own_low, own_high, ids_below, ids_above, ids_far = (
        lax.optimization_barrier(
            (below_low, above_high, own_low, own_high, ids_below, ids_above, ids_far)))
    below_high = shifted(own_high, "row", 1)
    above_low = shifted(own_low, "row", -1)
    far_low = shifted(below_low, "row", 1)
    far_high = shifted(above_high, "row", -1)

    slots_left_all = pair_left.reshape(piece_count, -1)
    slots_right_all = pair_right.reshape(piece_count, -1)
    counts_all = pair_count.reshape(piece_count)
    offsets = jnp.array([0, -1, 1, 2], jnp.int32)
    piece = (row_here + col_here + offsets) % piece_count
    left_id_stack = jnp.stack([own_ids, ids_below, ids_above, ids_far])
    right_id_stack = jnp.take(right_ids_pair, jnp.stack([col_here, 1 - col_here]), axis=0)
    pick = jnp.stack([1 - col_here, col_here]).astype(jnp.int32)
    slots_left = jnp.take(slots_left_all, piece, axis=0)
    slots_right = jnp.take(slots_right_all, piece, axis=0)
    right_of = jnp.array([0, 1, 1, 0], jnp.int32)
    places = (jnp.take_along_axis(left_id_stack, slots_left, axis=1) * slab_width
              + jnp.take_along_axis(right_id_stack[right_of], slots_right, axis=1))
    scalars = (slots_left, slots_right, jnp.take(counts_all, piece, axis=0), places, pick)
    totals = pair_products(scalars, (own_left, below_low, below_high, above_low, above_high,
                                     far_low, far_high, own_right, right_pair), targets)
    owned = lax.psum_scatter(totals, "layer", scatter_dimension=0, tiled=True)
    return owned.reshape(1, 1, -1, block_size, block_size)


def solution(mesh):
    in_specs = (
        P("row", "col", "layer", None, None, None),
        P("row", "col", "layer", None),
        P("row", "col", "layer", None, None, None),
        P("row", "col", "layer", None),
        P("row", "col", "layer", None, None),
        P("row", "col", "layer", None, None),
        P("row", "col", "layer", None),
    )
    out_specs = P("col", "row", "layer", None, None)
    return jax.shard_map(
        on_device, mesh=mesh, in_specs=in_specs, out_specs=out_specs, check_vma=False
    )
```

```python
import jax
import jax.numpy as jnp
from jax import lax
from jax.experimental import pallas as pl
from jax.experimental.pallas import tpu as pltpu
from jax.sharding import PartitionSpec as P

SLAB = 128
ROWS_GROUP = 8
UNROLL = 16


def pair_kernel(slots_left, slots_right, counts, left_ids, right_ids, pick,
                own_left, below_low, below_high, above_low, above_high, far_low, far_high,
                own_right, right_pair, totals, left_lists, right_lists, sems):
    half = far_low.shape[0]
    slab_width = totals.shape[0] // ROWS_GROUP
    block_size = totals.shape[-1]
    copies = [
        [pltpu.make_async_copy(own_left, left_lists.at[0], sems.at[0]),
         pltpu.make_async_copy(own_right, right_lists.at[0], sems.at[1])],
        [pltpu.make_async_copy(below_low, left_lists.at[1, pl.ds(0, half)], sems.at[2]),
         pltpu.make_async_copy(below_high, left_lists.at[1, pl.ds(half, half)], sems.at[7]),
         pltpu.make_async_copy(right_pair.at[pick[0]], right_lists.at[1], sems.at[3])],
        [pltpu.make_async_copy(above_low, left_lists.at[2, pl.ds(0, half)], sems.at[4]),
         pltpu.make_async_copy(above_high, left_lists.at[2, pl.ds(half, half)], sems.at[8])],
        [pltpu.make_async_copy(far_low, left_lists.at[3, pl.ds(0, half)], sems.at[5]),
         pltpu.make_async_copy(far_high, left_lists.at[3, pl.ds(half, half)], sems.at[6])],
    ]
    for group in copies:
        for copy in group:
            copy.start()

    def clear(t, carry):
        totals[t] = jnp.zeros((block_size, block_size), jnp.float32)
        return carry

    lax.fori_loop(0, totals.shape[0], clear, 0)

    for u, v in enumerate((0, 1, 1, 0)):
        for copy in copies[u]:
            copy.wait()

        def one_term(j, u=u, v=v):
            i = slots_left[u, j]
            k = slots_right[u, j]
            t = left_ids[u, i] * slab_width + right_ids[v, k]
            term = jnp.dot(left_lists[u, i], right_lists[v, k], preferred_element_type=jnp.float32)
            return t, term

        def add_group(g, carry, one_term=one_term):
            made = [one_term(g * UNROLL + q) for q in range(UNROLL)]
            for t, term in made:
                totals[t] = totals[t] + term
            return carry

        def add_single(j, carry, one_term=one_term):
            t, term = one_term(j)
            totals[t] = totals[t] + term
            return carry

        count = counts[u]
        groups = count // UNROLL
        lax.fori_loop(0, groups, add_group, 0)
        lax.fori_loop(groups * UNROLL, count, add_single, 0)


def pair_products(scalars, lists, targets):
    own_left = lists[0]
    list_cap, block_size = own_left.shape[0], own_left.shape[-1]
    smem = pl.BlockSpec(memory_space=pltpu.SMEM)
    hbm = pl.BlockSpec(memory_space=pl.ANY)
    return pl.pallas_call(
        pair_kernel,
        out_shape=jax.ShapeDtypeStruct((targets, block_size, block_size), jnp.float32),
        in_specs=[smem] * len(scalars) + [hbm] * len(lists),
        out_specs=pl.BlockSpec(memory_space=pltpu.VMEM),
        scratch_shapes=[
            pltpu.VMEM((4, list_cap, block_size, block_size), jnp.bfloat16),
            pltpu.VMEM((2, list_cap, block_size, block_size), jnp.bfloat16),
            pltpu.SemaphoreType.DMA((9,)),
        ],
        compiler_params=pltpu.CompilerParams(vmem_limit_bytes=60 * 1024 * 1024),
    )(*scalars, *lists)


def shifted(value, axis, steps):
    count = lax.axis_size(axis)
    pairs = [(source, (source + steps) % count) for source in range(count)]
    return lax.ppermute(value, axis, pairs)


def on_device(left_blocks, left_rows, right_blocks, right_cols, pair_left, pair_right, pair_count):
    block_size = left_blocks.shape[-1]
    left_cap = left_blocks.shape[3]
    right_cap = right_blocks.shape[3]
    piece_count = lax.axis_size("row")
    slab_width = SLAB // piece_count
    targets = ROWS_GROUP * slab_width
    row_here = lax.axis_index("row")
    col_here = lax.axis_index("col")
    own_left = left_blocks.reshape(left_cap, block_size, block_size)
    own_right = right_blocks.reshape(right_cap, block_size, block_size)
    own_ids = left_rows.reshape(left_cap)

    ids_below = shifted(own_ids, "row", 1)
    ids_above = shifted(own_ids, "row", -1)
    ids_far = shifted(own_ids, "row", 2)
    half = left_cap // 2
    own_low, own_high = own_left[:half], own_left[half:]
    below_low = shifted(own_low, "row", 1)
    above_high = shifted(own_high, "row", -1)
    right_pair = lax.all_gather(own_right, "col")
    right_ids_pair = lax.all_gather(right_cols.reshape(right_cap), "col")
    below_high = shifted(own_high, "row", 1)
    above_low = shifted(own_low, "row", -1)
    below_low, above_high, ids_below, ids_above, ids_far = lax.optimization_barrier(
        (below_low, above_high, ids_below, ids_above, ids_far))
    far_low = shifted(below_low, "row", 1)
    far_high = shifted(above_high, "row", -1)

    slots_left_all = pair_left.reshape(piece_count, -1)
    slots_right_all = pair_right.reshape(piece_count, -1)
    counts_all = pair_count.reshape(piece_count)
    offsets = jnp.array([0, -1, 1, 2], jnp.int32)
    piece = (row_here + col_here + offsets) % piece_count
    left_id_stack = jnp.stack([own_ids, ids_below, ids_above, ids_far])
    right_id_stack = jnp.take(right_ids_pair, jnp.stack([col_here, 1 - col_here]), axis=0)
    pick = jnp.stack([1 - col_here, col_here]).astype(jnp.int32)
    scalars = (jnp.take(slots_left_all, piece, axis=0), jnp.take(slots_right_all, piece, axis=0),
               jnp.take(counts_all, piece, axis=0), left_id_stack, right_id_stack, pick)
    totals = pair_products(scalars, (own_left, below_low, below_high, above_low, above_high,
                                     far_low, far_high, own_right, right_pair), targets)
    owned = lax.psum_scatter(totals, "layer", scatter_dimension=0, tiled=True)
    return owned.reshape(1, 1, -1, block_size, block_size)


def solution(mesh):
    in_specs = (
        P("row", "col", "layer", None, None, None),
        P("row", "col", "layer", None),
        P("row", "col", "layer", None, None, None),
        P("row", "col", "layer", None),
        P("row", "col", "layer", None, None),
        P("row", "col", "layer", None, None),
        P("row", "col", "layer", None),
    )
    out_specs = P("col", "row", "layer", None, None)
    return jax.shard_map(
        on_device, mesh=mesh, in_specs=in_specs, out_specs=out_specs, check_vma=False
    )
```

```python
import jax
import jax.numpy as jnp
from jax import lax
from jax.experimental import pallas as pl
from jax.experimental.pallas import tpu as pltpu
from jax.sharding import PartitionSpec as P

SLAB = 128
ROWS_GROUP = 8
UNROLL = 16


def pair_kernel(slots_left, slots_right, counts, left_ids, right_ids, pick, order, bounds,
                own_left, below_low, below_high, above_low, above_high, far_low, far_high,
                own_right, right_pair, out, totals, left_lists, right_lists, sems, out_sem):
    half = far_low.shape[0]
    slab_width = totals.shape[0] // ROWS_GROUP
    block_size = totals.shape[-1]
    copies = [
        [pltpu.make_async_copy(own_left, left_lists.at[0], sems.at[0]),
         pltpu.make_async_copy(own_right, right_lists.at[0], sems.at[1])],
        [pltpu.make_async_copy(below_low, left_lists.at[1, pl.ds(0, half)], sems.at[2]),
         pltpu.make_async_copy(below_high, left_lists.at[1, pl.ds(half, half)], sems.at[7]),
         pltpu.make_async_copy(right_pair.at[pick[0]], right_lists.at[1], sems.at[3])],
        [pltpu.make_async_copy(above_low, left_lists.at[2, pl.ds(0, half)], sems.at[4]),
         pltpu.make_async_copy(above_high, left_lists.at[2, pl.ds(half, half)], sems.at[8])],
        [pltpu.make_async_copy(far_low, left_lists.at[3, pl.ds(0, half)], sems.at[5]),
         pltpu.make_async_copy(far_high, left_lists.at[3, pl.ds(half, half)], sems.at[6])],
    ]
    for group in copies:
        for copy in group:
            copy.start()

    def clear(t, carry):
        totals[t] = jnp.zeros((block_size, block_size), jnp.float32)
        return carry

    lax.fori_loop(0, totals.shape[0], clear, 0)

    def flush(group):
        def one(n, carry):
            t = order[n]
            pltpu.make_async_copy(totals.at[t], out.at[t], out_sem.at[0]).start()
            return carry

        lax.fori_loop(bounds[group], bounds[group + 1], one, 0)

    flush(0)

    for u, v in enumerate((0, 1, 1, 0)):
        for copy in copies[u]:
            copy.wait()

        def one_term(j, u=u, v=v):
            i = slots_left[u, j]
            k = slots_right[u, j]
            t = left_ids[u, i] * slab_width + right_ids[v, k]
            term = jnp.dot(left_lists[u, i], right_lists[v, k], preferred_element_type=jnp.float32)
            return t, term

        def add_group(g, carry, one_term=one_term):
            made = [one_term(g * UNROLL + q) for q in range(UNROLL)]
            for t, term in made:
                totals[t] = totals[t] + term
            return carry

        def add_single(j, carry, one_term=one_term):
            t, term = one_term(j)
            totals[t] = totals[t] + term
            return carry

        count = counts[u]
        groups = count // UNROLL
        lax.fori_loop(0, groups, add_group, 0)
        lax.fori_loop(groups * UNROLL, count, add_single, 0)
        flush(u + 1)

    pltpu.make_async_copy(totals, out, out_sem.at[0]).wait()


def pair_products(scalars, lists, targets):
    own_left = lists[0]
    list_cap, block_size = own_left.shape[0], own_left.shape[-1]
    smem = pl.BlockSpec(memory_space=pltpu.SMEM)
    hbm = pl.BlockSpec(memory_space=pl.ANY)
    return pl.pallas_call(
        pair_kernel,
        out_shape=jax.ShapeDtypeStruct((targets, block_size, block_size), jnp.float32),
        in_specs=[smem] * len(scalars) + [hbm] * len(lists),
        out_specs=hbm,
        scratch_shapes=[
            pltpu.VMEM((targets, block_size, block_size), jnp.float32),
            pltpu.VMEM((4, list_cap, block_size, block_size), jnp.bfloat16),
            pltpu.VMEM((2, list_cap, block_size, block_size), jnp.bfloat16),
            pltpu.SemaphoreType.DMA((9,)),
            pltpu.SemaphoreType.DMA((1,)),
        ],
        compiler_params=pltpu.CompilerParams(vmem_limit_bytes=60 * 1024 * 1024),
    )(*scalars, *lists)


def shifted(value, axis, steps):
    count = lax.axis_size(axis)
    pairs = [(source, (source + steps) % count) for source in range(count)]
    return lax.ppermute(value, axis, pairs)


def on_device(left_blocks, left_rows, right_blocks, right_cols, pair_left, pair_right, pair_count):
    block_size = left_blocks.shape[-1]
    left_cap = left_blocks.shape[3]
    right_cap = right_blocks.shape[3]
    piece_count = lax.axis_size("row")
    slab_width = SLAB // piece_count
    targets = ROWS_GROUP * slab_width
    row_here = lax.axis_index("row")
    col_here = lax.axis_index("col")
    own_left = left_blocks.reshape(left_cap, block_size, block_size)
    own_right = right_blocks.reshape(right_cap, block_size, block_size)
    own_ids = left_rows.reshape(left_cap)

    ids_below = shifted(own_ids, "row", 1)
    ids_above = shifted(own_ids, "row", -1)
    ids_far = shifted(own_ids, "row", 2)
    half = left_cap // 2
    own_low, own_high = own_left[:half], own_left[half:]
    below_low = shifted(own_low, "row", 1)
    above_high = shifted(own_high, "row", -1)
    right_pair = lax.all_gather(own_right, "col")
    right_ids_pair = lax.all_gather(right_cols.reshape(right_cap), "col")
    below_low, above_high, own_low, own_high, ids_below, ids_above, ids_far = (
        lax.optimization_barrier(
            (below_low, above_high, own_low, own_high, ids_below, ids_above, ids_far)))
    below_high = shifted(own_high, "row", 1)
    above_low = shifted(own_low, "row", -1)
    far_low = shifted(below_low, "row", 1)
    far_high = shifted(above_high, "row", -1)

    slots_left_all = pair_left.reshape(piece_count, -1)
    slots_right_all = pair_right.reshape(piece_count, -1)
    counts_all = pair_count.reshape(piece_count)
    offsets = jnp.array([0, -1, 1, 2], jnp.int32)
    piece = (row_here + col_here + offsets) % piece_count
    left_id_stack = jnp.stack([own_ids, ids_below, ids_above, ids_far])
    right_id_stack = jnp.take(right_ids_pair, jnp.stack([col_here, 1 - col_here]), axis=0)
    pick = jnp.stack([1 - col_here, col_here]).astype(jnp.int32)
    slots_left = jnp.take(slots_left_all, piece, axis=0)
    slots_right = jnp.take(slots_right_all, piece, axis=0)
    counts = jnp.take(counts_all, piece, axis=0)
    right_of = jnp.array([0, 1, 1, 0], jnp.int32)
    places = (jnp.take_along_axis(left_id_stack, slots_left, axis=1) * slab_width
              + jnp.take_along_axis(right_id_stack[right_of], slots_right, axis=1))
    live = jnp.arange(slots_left.shape[1], dtype=jnp.int32)[None, :] < counts[:, None]
    lists = jnp.arange(4, dtype=jnp.int32)[:, None] + jnp.zeros_like(places)
    last = jnp.full((targets,), -1, jnp.int32).at[places.reshape(-1)].max(
        jnp.where(live, lists, -1).reshape(-1))
    member = (last[:, None] == jnp.arange(-1, 4, dtype=jnp.int32)[None, :]).astype(jnp.int32)
    sizes = member.sum(axis=0)
    bounds = jnp.concatenate([jnp.zeros((1,), jnp.int32), jnp.cumsum(sizes)]).astype(jnp.int32)
    rank = jnp.sum((jnp.cumsum(member, axis=0) - 1) * member, axis=1)
    slot = jnp.take(bounds, last + 1) + rank
    order = jnp.zeros((targets,), jnp.int32).at[slot].set(jnp.arange(targets, dtype=jnp.int32))
    scalars = (slots_left, slots_right, counts, left_id_stack, right_id_stack, pick, order, bounds)
    totals = pair_products(scalars, (own_left, below_low, below_high, above_low, above_high,
                                     far_low, far_high, own_right, right_pair), targets)
    owned = lax.psum_scatter(totals, "layer", scatter_dimension=0, tiled=True)
    return owned.reshape(1, 1, -1, block_size, block_size)


def solution(mesh):
    in_specs = (
        P("row", "col", "layer", None, None, None),
        P("row", "col", "layer", None),
        P("row", "col", "layer", None, None, None),
        P("row", "col", "layer", None),
        P("row", "col", "layer", None, None),
        P("row", "col", "layer", None, None),
        P("row", "col", "layer", None),
    )
    out_specs = P("col", "row", "layer", None, None)
    return jax.shard_map(
        on_device, mesh=mesh, in_specs=in_specs, out_specs=out_specs, check_vma=False
    )
```

```python
import jax
import jax.numpy as jnp
from jax import lax
from jax.experimental import pallas as pl
from jax.experimental.pallas import tpu as pltpu
from jax.sharding import PartitionSpec as P

SLAB = 128
ROWS_GROUP = 8
UNROLL = 16


def pair_kernel(slots_left, slots_right, counts, left_ids, right_ids, pick, order, bounds,
                own_left, below_low, below_high, above_low, above_high, far_low, far_high,
                own_right, right_pair, out, totals, left_lists, right_lists, sems, out_sem):
    half = far_low.shape[0]
    slab_width = totals.shape[0] // ROWS_GROUP
    block_size = totals.shape[-1]
    copies = [
        [pltpu.make_async_copy(own_left, left_lists.at[0], sems.at[0]),
         pltpu.make_async_copy(own_right, right_lists.at[0], sems.at[1])],
        [pltpu.make_async_copy(below_low, left_lists.at[1, pl.ds(0, half)], sems.at[2]),
         pltpu.make_async_copy(below_high, left_lists.at[1, pl.ds(half, half)], sems.at[7]),
         pltpu.make_async_copy(right_pair.at[pick[0]], right_lists.at[1], sems.at[3])],
        [pltpu.make_async_copy(above_low, left_lists.at[2, pl.ds(0, half)], sems.at[4]),
         pltpu.make_async_copy(above_high, left_lists.at[2, pl.ds(half, half)], sems.at[8])],
        [pltpu.make_async_copy(far_low, left_lists.at[3, pl.ds(0, half)], sems.at[5]),
         pltpu.make_async_copy(far_high, left_lists.at[3, pl.ds(half, half)], sems.at[6])],
    ]
    for group in copies:
        for copy in group:
            copy.start()

    def clear(t, carry):
        totals[t] = jnp.zeros((block_size, block_size), jnp.float32)
        return carry

    lax.fori_loop(0, totals.shape[0], clear, 0)

    def flush(group):
        def one(n, carry):
            t = order[n]
            pltpu.make_async_copy(totals.at[t], out.at[t], out_sem.at[0]).start()
            return carry

        lax.fori_loop(bounds[group], bounds[group + 1], one, 0)

    flush(0)

    for u, v in enumerate((0, 1, 1, 0)):
        for copy in copies[u]:
            copy.wait()

        def one_term(j, u=u, v=v):
            i = slots_left[u, j]
            k = slots_right[u, j]
            t = left_ids[u, i] * slab_width + right_ids[v, k]
            term = jnp.dot(left_lists[u, i], right_lists[v, k], preferred_element_type=jnp.float32)
            return t, term

        def add_group(g, carry, one_term=one_term):
            made = [one_term(g * UNROLL + q) for q in range(UNROLL)]
            for t, term in made:
                totals[t] = totals[t] + term
            return carry

        def add_single(j, carry, one_term=one_term):
            t, term = one_term(j)
            totals[t] = totals[t] + term
            return carry

        count = counts[u]
        groups = count // UNROLL
        lax.fori_loop(0, groups, add_group, 0)
        lax.fori_loop(groups * UNROLL, count, add_single, 0)
        flush(u + 1)

    pltpu.make_async_copy(totals, out, out_sem.at[0]).wait()


def pair_products(scalars, lists, targets):
    own_left = lists[0]
    list_cap, block_size = own_left.shape[0], own_left.shape[-1]
    smem = pl.BlockSpec(memory_space=pltpu.SMEM)
    hbm = pl.BlockSpec(memory_space=pl.ANY)
    return pl.pallas_call(
        pair_kernel,
        out_shape=jax.ShapeDtypeStruct((targets, block_size, block_size), jnp.float32),
        in_specs=[smem] * len(scalars) + [hbm] * len(lists),
        out_specs=hbm,
        scratch_shapes=[
            pltpu.VMEM((targets, block_size, block_size), jnp.float32),
            pltpu.VMEM((4, list_cap, block_size, block_size), jnp.bfloat16),
            pltpu.VMEM((2, list_cap, block_size, block_size), jnp.bfloat16),
            pltpu.SemaphoreType.DMA((9,)),
            pltpu.SemaphoreType.DMA((1,)),
        ],
        compiler_params=pltpu.CompilerParams(vmem_limit_bytes=60 * 1024 * 1024),
    )(*scalars, *lists)


def shifted(value, axis, steps):
    count = lax.axis_size(axis)
    pairs = [(source, (source + steps) % count) for source in range(count)]
    return lax.ppermute(value, axis, pairs)


def on_device(left_blocks, left_rows, right_blocks, right_cols, pair_left, pair_right, pair_count):
    block_size = left_blocks.shape[-1]
    left_cap = left_blocks.shape[3]
    right_cap = right_blocks.shape[3]
    piece_count = lax.axis_size("row")
    slab_width = SLAB // piece_count
    targets = ROWS_GROUP * slab_width
    row_here = lax.axis_index("row")
    col_here = lax.axis_index("col")
    own_left = left_blocks.reshape(left_cap, block_size, block_size)
    own_right = right_blocks.reshape(right_cap, block_size, block_size)
    own_ids = left_rows.reshape(left_cap)

    ids_below = shifted(own_ids, "row", 1)
    ids_above = shifted(own_ids, "row", -1)
    ids_far = shifted(own_ids, "row", 2)
    half = left_cap // 2
    own_low, own_high = own_left[:half], own_left[half:]
    below_low = shifted(own_low, "row", 1)
    above_high = shifted(own_high, "row", -1)
    right_pair = lax.all_gather(own_right, "col")
    right_ids_pair = lax.all_gather(right_cols.reshape(right_cap), "col")
    below_low, above_high, own_low, own_high, ids_below, ids_above, ids_far = (
        lax.optimization_barrier(
            (below_low, above_high, own_low, own_high, ids_below, ids_above, ids_far)))
    below_high = shifted(own_high, "row", 1)
    above_low = shifted(own_low, "row", -1)
    far_low = shifted(below_low, "row", 1)
    far_high = shifted(above_high, "row", -1)

    slots_left_all = pair_left.reshape(piece_count, -1)
    slots_right_all = pair_right.reshape(piece_count, -1)
    counts_all = pair_count.reshape(piece_count)
    offsets = jnp.array([0, -1, 1, 2], jnp.int32)
    piece = (row_here + col_here + offsets) % piece_count
    left_id_stack = jnp.stack([own_ids, ids_below, ids_above, ids_far])
    right_id_stack = jnp.take(right_ids_pair, jnp.stack([col_here, 1 - col_here]), axis=0)
    pick = jnp.stack([1 - col_here, col_here]).astype(jnp.int32)
    below_high, left_id_stack, right_id_stack, slots_left_all, slots_right_all, counts_all = (
        lax.optimization_barrier((below_high, left_id_stack, right_id_stack, slots_left_all,
                                  slots_right_all, counts_all)))
    slots_left = jnp.take(slots_left_all, piece, axis=0)
    slots_right = jnp.take(slots_right_all, piece, axis=0)
    counts = jnp.take(counts_all, piece, axis=0)
    right_of = jnp.array([0, 1, 1, 0], jnp.int32)
    places = (jnp.take_along_axis(left_id_stack, slots_left, axis=1) * slab_width
              + jnp.take_along_axis(right_id_stack[right_of], slots_right, axis=1))
    live = jnp.arange(slots_left.shape[1], dtype=jnp.int32)[None, :] < counts[:, None]
    lists = jnp.arange(4, dtype=jnp.int32)[:, None] + jnp.zeros_like(places)
    last = jnp.full((targets,), -1, jnp.int32).at[places.reshape(-1)].max(
        jnp.where(live, lists, -1).reshape(-1))
    member = (last[:, None] == jnp.arange(-1, 4, dtype=jnp.int32)[None, :]).astype(jnp.int32)
    sizes = member.sum(axis=0)
    bounds = jnp.concatenate([jnp.zeros((1,), jnp.int32), jnp.cumsum(sizes)]).astype(jnp.int32)
    rank = jnp.sum((jnp.cumsum(member, axis=0) - 1) * member, axis=1)
    slot = jnp.take(bounds, last + 1) + rank
    order = jnp.zeros((targets,), jnp.int32).at[slot].set(jnp.arange(targets, dtype=jnp.int32))
    scalars = (slots_left, slots_right, counts, left_id_stack, right_id_stack, pick, order, bounds)
    totals = pair_products(scalars, (own_left, below_low, below_high, above_low, above_high,
                                     far_low, far_high, own_right, right_pair), targets)
    owned = lax.psum_scatter(totals, "layer", scatter_dimension=0, tiled=True)
    return owned.reshape(1, 1, -1, block_size, block_size)


def solution(mesh):
    in_specs = (
        P("row", "col", "layer", None, None, None),
        P("row", "col", "layer", None),
        P("row", "col", "layer", None, None, None),
        P("row", "col", "layer", None),
        P("row", "col", "layer", None, None),
        P("row", "col", "layer", None, None),
        P("row", "col", "layer", None),
    )
    out_specs = P("col", "row", "layer", None, None)
    return jax.shard_map(
        on_device, mesh=mesh, in_specs=in_specs, out_specs=out_specs, check_vma=False
    )
```

```python
import jax
import jax.numpy as jnp
from jax import lax
from jax.experimental import pallas as pl
from jax.experimental.pallas import tpu as pltpu
from jax.sharding import PartitionSpec as P

SLAB = 128
ROWS_GROUP = 8
UNROLL = 16


def pair_kernel(slots_left, slots_right, counts, left_ids, right_ids, pick,
                own_left, below_low, below_high, above_low, above_high, far_low, far_high,
                own_right, right_pair, out, totals, left_lists, right_lists, sems, out_sem, touched):
    half = far_low.shape[0]
    slab_width = totals.shape[0] // ROWS_GROUP
    block_size = totals.shape[-1]
    copies = [
        [pltpu.make_async_copy(own_left, left_lists.at[0], sems.at[0]),
         pltpu.make_async_copy(own_right, right_lists.at[0], sems.at[1])],
        [pltpu.make_async_copy(below_low, left_lists.at[1, pl.ds(0, half)], sems.at[2]),
         pltpu.make_async_copy(below_high, left_lists.at[1, pl.ds(half, half)], sems.at[7]),
         pltpu.make_async_copy(right_pair.at[pick[0]], right_lists.at[1], sems.at[3])],
        [pltpu.make_async_copy(above_low, left_lists.at[2, pl.ds(0, half)], sems.at[4]),
         pltpu.make_async_copy(above_high, left_lists.at[2, pl.ds(half, half)], sems.at[8])],
        [pltpu.make_async_copy(far_low, left_lists.at[3, pl.ds(0, half)], sems.at[5]),
         pltpu.make_async_copy(far_high, left_lists.at[3, pl.ds(half, half)], sems.at[6])],
    ]
    for group in copies:
        for copy in group:
            copy.start()

    def clear(t, carry):
        totals[t] = jnp.zeros((block_size, block_size), jnp.float32)
        return carry

    lax.fori_loop(0, totals.shape[0], clear, 0)

    def unmark(t, carry):
        touched[t] = 0
        return carry

    lax.fori_loop(0, totals.shape[0], unmark, 0)

    def mark(j, carry):
        t = left_ids[3, slots_left[3, j]] * slab_width + right_ids[0, slots_right[3, j]]
        touched[t] = 1
        return carry

    lax.fori_loop(0, counts[3], mark, 0)

    def flush(flag):
        def one(t, carry):
            @pl.when(touched[t] == flag)
            def _():
                pltpu.make_async_copy(totals.at[t], out.at[t], out_sem.at[0]).start()
            return carry

        lax.fori_loop(0, totals.shape[0], one, 0)

    for u, v in enumerate((0, 1, 1, 0)):
        for copy in copies[u]:
            copy.wait()

        def one_term(j, u=u, v=v):
            i = slots_left[u, j]
            k = slots_right[u, j]
            t = left_ids[u, i] * slab_width + right_ids[v, k]
            term = jnp.dot(left_lists[u, i], right_lists[v, k], preferred_element_type=jnp.float32)
            return t, term

        def add_group(g, carry, one_term=one_term):
            made = [one_term(g * UNROLL + q) for q in range(UNROLL)]
            for t, term in made:
                totals[t] = totals[t] + term
            return carry

        def add_single(j, carry, one_term=one_term):
            t, term = one_term(j)
            totals[t] = totals[t] + term
            return carry

        count = counts[u]
        groups = count // UNROLL
        lax.fori_loop(0, groups, add_group, 0)
        lax.fori_loop(groups * UNROLL, count, add_single, 0)
        if u >= 2:
            flush(u - 2)

    pltpu.make_async_copy(totals, out, out_sem.at[0]).wait()


def pair_products(scalars, lists, targets):
    own_left = lists[0]
    list_cap, block_size = own_left.shape[0], own_left.shape[-1]
    smem = pl.BlockSpec(memory_space=pltpu.SMEM)
    hbm = pl.BlockSpec(memory_space=pl.ANY)
    return pl.pallas_call(
        pair_kernel,
        out_shape=jax.ShapeDtypeStruct((targets, block_size, block_size), jnp.float32),
        in_specs=[smem] * len(scalars) + [hbm] * len(lists),
        out_specs=hbm,
        scratch_shapes=[
            pltpu.VMEM((targets, block_size, block_size), jnp.float32),
            pltpu.VMEM((4, list_cap, block_size, block_size), jnp.bfloat16),
            pltpu.VMEM((2, list_cap, block_size, block_size), jnp.bfloat16),
            pltpu.SemaphoreType.DMA((9,)),
            pltpu.SemaphoreType.DMA((1,)),
            pltpu.SMEM((targets,), jnp.int32),
        ],
        compiler_params=pltpu.CompilerParams(vmem_limit_bytes=60 * 1024 * 1024),
    )(*scalars, *lists)


def shifted(value, axis, steps):
    count = lax.axis_size(axis)
    pairs = [(source, (source + steps) % count) for source in range(count)]
    return lax.ppermute(value, axis, pairs)


def on_device(left_blocks, left_rows, right_blocks, right_cols, pair_left, pair_right, pair_count):
    block_size = left_blocks.shape[-1]
    left_cap = left_blocks.shape[3]
    right_cap = right_blocks.shape[3]
    piece_count = lax.axis_size("row")
    slab_width = SLAB // piece_count
    targets = ROWS_GROUP * slab_width
    row_here = lax.axis_index("row")
    col_here = lax.axis_index("col")
    own_left = left_blocks.reshape(left_cap, block_size, block_size)
    own_right = right_blocks.reshape(right_cap, block_size, block_size)
    own_ids = left_rows.reshape(left_cap)

    ids_below = shifted(own_ids, "row", 1)
    ids_above = shifted(own_ids, "row", -1)
    ids_far = shifted(own_ids, "row", 2)
    half = left_cap // 2
    own_low, own_high = own_left[:half], own_left[half:]
    below_low = shifted(own_low, "row", 1)
    above_high = shifted(own_high, "row", -1)
    right_pair = lax.all_gather(own_right, "col")
    right_ids_pair = lax.all_gather(right_cols.reshape(right_cap), "col")
    below_low, above_high, own_low, own_high, ids_below, ids_above, ids_far = (
        lax.optimization_barrier(
            (below_low, above_high, own_low, own_high, ids_below, ids_above, ids_far)))
    below_high = shifted(own_high, "row", 1)
    above_low = shifted(own_low, "row", -1)
    far_low = shifted(below_low, "row", 1)
    far_high = shifted(above_high, "row", -1)

    slots_left_all = pair_left.reshape(piece_count, -1)
    slots_right_all = pair_right.reshape(piece_count, -1)
    counts_all = pair_count.reshape(piece_count)
    offsets = jnp.array([0, -1, 1, 2], jnp.int32)
    piece = (row_here + col_here + offsets) % piece_count
    left_id_stack = jnp.stack([own_ids, ids_below, ids_above, ids_far])
    right_id_stack = jnp.take(right_ids_pair, jnp.stack([col_here, 1 - col_here]), axis=0)
    pick = jnp.stack([1 - col_here, col_here]).astype(jnp.int32)
    scalars = (jnp.take(slots_left_all, piece, axis=0), jnp.take(slots_right_all, piece, axis=0),
               jnp.take(counts_all, piece, axis=0), left_id_stack, right_id_stack, pick)
    totals = pair_products(scalars, (own_left, below_low, below_high, above_low, above_high,
                                     far_low, far_high, own_right, right_pair), targets)
    owned = lax.psum_scatter(totals, "layer", scatter_dimension=0, tiled=True)
    return owned.reshape(1, 1, -1, block_size, block_size)


def solution(mesh):
    in_specs = (
        P("row", "col", "layer", None, None, None),
        P("row", "col", "layer", None),
        P("row", "col", "layer", None, None, None),
        P("row", "col", "layer", None),
        P("row", "col", "layer", None, None),
        P("row", "col", "layer", None, None),
        P("row", "col", "layer", None),
    )
    out_specs = P("col", "row", "layer", None, None)
    return jax.shard_map(
        on_device, mesh=mesh, in_specs=in_specs, out_specs=out_specs, check_vma=False
    )
```

```python
import jax
import jax.numpy as jnp
from jax import lax
from jax.experimental import pallas as pl
from jax.experimental.pallas import tpu as pltpu
from jax.sharding import PartitionSpec as P

SLAB = 128
ROWS_GROUP = 8
UNROLL = 16


def pair_kernel(slots_left, slots_right, counts, left_ids, right_ids, pick,
                own_left, below_low, below_high, above_low, above_high, far_low, far_high,
                own_right, right_pair, out, totals, left_lists, right_lists, sems, out_sems):
    half = far_low.shape[0]
    slab_width = totals.shape[0] // ROWS_GROUP
    block_size = totals.shape[-1]
    copies = [
        [pltpu.make_async_copy(own_left, left_lists.at[0], sems.at[0]),
         pltpu.make_async_copy(own_right, right_lists.at[0], sems.at[1])],
        [pltpu.make_async_copy(below_low, left_lists.at[1, pl.ds(0, half)], sems.at[2]),
         pltpu.make_async_copy(below_high, left_lists.at[1, pl.ds(half, half)], sems.at[7]),
         pltpu.make_async_copy(right_pair.at[pick[0]], right_lists.at[1], sems.at[3])],
        [pltpu.make_async_copy(above_low, left_lists.at[2, pl.ds(0, half)], sems.at[4]),
         pltpu.make_async_copy(above_high, left_lists.at[2, pl.ds(half, half)], sems.at[8])],
        [pltpu.make_async_copy(far_low, left_lists.at[3, pl.ds(0, half)], sems.at[5]),
         pltpu.make_async_copy(far_high, left_lists.at[3, pl.ds(half, half)], sems.at[6])],
    ]
    for group in copies:
        for copy in group:
            copy.start()

    def clear(t, carry):
        totals[t] = jnp.zeros((block_size, block_size), jnp.float32)
        return carry

    lax.fori_loop(0, totals.shape[0], clear, 0)

    for u, v in enumerate((0, 1, 1, 0)):
        for copy in copies[u]:
            copy.wait()

        def one_term(j, u=u, v=v):
            i = slots_left[u, j]
            k = slots_right[u, j]
            t = left_ids[u, i] * slab_width + right_ids[v, k]
            term = jnp.dot(left_lists[u, i], right_lists[v, k], preferred_element_type=jnp.float32)
            return t, term

        def add_group(g, carry, one_term=one_term):
            made = [one_term(g * UNROLL + q) for q in range(UNROLL)]
            for t, term in made:
                totals[t] = totals[t] + term
            return carry

        def add_single(j, carry, one_term=one_term):
            t, term = one_term(j)
            totals[t] = totals[t] + term
            return carry

        count = counts[u]
        groups = count // UNROLL
        lax.fori_loop(0, groups, add_group, 0)
        lax.fori_loop(groups * UNROLL, count, add_single, 0)

    part = totals.shape[0] // 4
    out_copies = [pltpu.make_async_copy(totals.at[pl.ds(q * part, part)],
                                        out.at[pl.ds(q * part, part)], out_sems.at[q])
                  for q in range(4)]
    for copy in out_copies:
        copy.start()
    for copy in out_copies:
        copy.wait()


def pair_products(scalars, lists, targets):
    own_left = lists[0]
    list_cap, block_size = own_left.shape[0], own_left.shape[-1]
    smem = pl.BlockSpec(memory_space=pltpu.SMEM)
    hbm = pl.BlockSpec(memory_space=pl.ANY)
    return pl.pallas_call(
        pair_kernel,
        out_shape=jax.ShapeDtypeStruct((targets, block_size, block_size), jnp.float32),
        in_specs=[smem] * len(scalars) + [hbm] * len(lists),
        out_specs=hbm,
        scratch_shapes=[
            pltpu.VMEM((targets, block_size, block_size), jnp.float32),
            pltpu.VMEM((4, list_cap, block_size, block_size), jnp.bfloat16),
            pltpu.VMEM((2, list_cap, block_size, block_size), jnp.bfloat16),
            pltpu.SemaphoreType.DMA((9,)),
            pltpu.SemaphoreType.DMA((4,)),
        ],
        compiler_params=pltpu.CompilerParams(vmem_limit_bytes=60 * 1024 * 1024),
    )(*scalars, *lists)


def shifted(value, axis, steps):
    count = lax.axis_size(axis)
    pairs = [(source, (source + steps) % count) for source in range(count)]
    return lax.ppermute(value, axis, pairs)


def on_device(left_blocks, left_rows, right_blocks, right_cols, pair_left, pair_right, pair_count):
    block_size = left_blocks.shape[-1]
    left_cap = left_blocks.shape[3]
    right_cap = right_blocks.shape[3]
    piece_count = lax.axis_size("row")
    slab_width = SLAB // piece_count
    targets = ROWS_GROUP * slab_width
    row_here = lax.axis_index("row")
    col_here = lax.axis_index("col")
    own_left = left_blocks.reshape(left_cap, block_size, block_size)
    own_right = right_blocks.reshape(right_cap, block_size, block_size)
    own_ids = left_rows.reshape(left_cap)

    ids_below = shifted(own_ids, "row", 1)
    ids_above = shifted(own_ids, "row", -1)
    ids_far = shifted(own_ids, "row", 2)
    half = left_cap // 2
    own_low, own_high = own_left[:half], own_left[half:]
    below_low = shifted(own_low, "row", 1)
    above_high = shifted(own_high, "row", -1)
    right_pair = lax.all_gather(own_right, "col")
    right_ids_pair = lax.all_gather(right_cols.reshape(right_cap), "col")
    below_low, above_high, own_low, own_high, ids_below, ids_above, ids_far = (
        lax.optimization_barrier(
            (below_low, above_high, own_low, own_high, ids_below, ids_above, ids_far)))
    below_high = shifted(own_high, "row", 1)
    above_low = shifted(own_low, "row", -1)
    far_low = shifted(below_low, "row", 1)
    far_high = shifted(above_high, "row", -1)

    slots_left_all = pair_left.reshape(piece_count, -1)
    slots_right_all = pair_right.reshape(piece_count, -1)
    counts_all = pair_count.reshape(piece_count)
    offsets = jnp.array([0, -1, 1, 2], jnp.int32)
    piece = (row_here + col_here + offsets) % piece_count
    left_id_stack = jnp.stack([own_ids, ids_below, ids_above, ids_far])
    right_id_stack = jnp.take(right_ids_pair, jnp.stack([col_here, 1 - col_here]), axis=0)
    pick = jnp.stack([1 - col_here, col_here]).astype(jnp.int32)
    scalars = (jnp.take(slots_left_all, piece, axis=0), jnp.take(slots_right_all, piece, axis=0),
               jnp.take(counts_all, piece, axis=0), left_id_stack, right_id_stack, pick)
    totals = pair_products(scalars, (own_left, below_low, below_high, above_low, above_high,
                                     far_low, far_high, own_right, right_pair), targets)
    owned = lax.psum_scatter(totals, "layer", scatter_dimension=0, tiled=True)
    return owned.reshape(1, 1, -1, block_size, block_size)


def solution(mesh):
    in_specs = (
        P("row", "col", "layer", None, None, None),
        P("row", "col", "layer", None),
        P("row", "col", "layer", None, None, None),
        P("row", "col", "layer", None),
        P("row", "col", "layer", None, None),
        P("row", "col", "layer", None, None),
        P("row", "col", "layer", None),
    )
    out_specs = P("col", "row", "layer", None, None)
    return jax.shard_map(
        on_device, mesh=mesh, in_specs=in_specs, out_specs=out_specs, check_vma=False
    )
```

```python
import jax
import jax.numpy as jnp
from jax import lax
from jax.experimental import pallas as pl
from jax.experimental.pallas import tpu as pltpu
from jax.sharding import PartitionSpec as P

SLAB = 128
ROWS_GROUP = 8
UNROLL = 20


def pair_kernel(slots_left, slots_right, counts, left_ids, right_ids, pick,
                own_left, below_low, below_high, above_low, above_high, far_low, far_high,
                own_right, right_pair, totals, left_lists, right_lists, sems):
    half = far_low.shape[0]
    slab_width = totals.shape[0] // ROWS_GROUP
    block_size = totals.shape[-1]
    copies = [
        [pltpu.make_async_copy(own_left, left_lists.at[0], sems.at[0]),
         pltpu.make_async_copy(own_right, right_lists.at[0], sems.at[1])],
        [pltpu.make_async_copy(below_low, left_lists.at[1, pl.ds(0, half)], sems.at[2]),
         pltpu.make_async_copy(below_high, left_lists.at[1, pl.ds(half, half)], sems.at[7]),
         pltpu.make_async_copy(right_pair.at[pick[0]], right_lists.at[1], sems.at[3])],
        [pltpu.make_async_copy(above_low, left_lists.at[2, pl.ds(0, half)], sems.at[4]),
         pltpu.make_async_copy(above_high, left_lists.at[2, pl.ds(half, half)], sems.at[8])],
        [pltpu.make_async_copy(far_low, left_lists.at[3, pl.ds(0, half)], sems.at[5]),
         pltpu.make_async_copy(far_high, left_lists.at[3, pl.ds(half, half)], sems.at[6])],
    ]
    for group in copies:
        for copy in group:
            copy.start()

    def clear(t, carry):
        totals[t] = jnp.zeros((block_size, block_size), jnp.float32)
        return carry

    lax.fori_loop(0, totals.shape[0], clear, 0)

    for u, v in enumerate((0, 1, 1, 0)):
        for copy in copies[u]:
            copy.wait()

        def one_term(j, u=u, v=v):
            i = slots_left[u, j]
            k = slots_right[u, j]
            t = left_ids[u, i] * slab_width + right_ids[v, k]
            term = jnp.dot(left_lists[u, i], right_lists[v, k], preferred_element_type=jnp.float32)
            return t, term

        def add_group(g, carry, one_term=one_term):
            made = [one_term(g * UNROLL + q) for q in range(UNROLL)]
            for t, term in made:
                totals[t] = totals[t] + term
            return carry

        def add_single(j, carry, one_term=one_term):
            t, term = one_term(j)
            totals[t] = totals[t] + term
            return carry

        count = counts[u]
        groups = count // UNROLL
        lax.fori_loop(0, groups, add_group, 0)
        lax.fori_loop(groups * UNROLL, count, add_single, 0)


def pair_products(scalars, lists, targets):
    own_left = lists[0]
    list_cap, block_size = own_left.shape[0], own_left.shape[-1]
    smem = pl.BlockSpec(memory_space=pltpu.SMEM)
    hbm = pl.BlockSpec(memory_space=pl.ANY)
    return pl.pallas_call(
        pair_kernel,
        out_shape=jax.ShapeDtypeStruct((targets, block_size, block_size), jnp.float32),
        in_specs=[smem] * len(scalars) + [hbm] * len(lists),
        out_specs=pl.BlockSpec(memory_space=pltpu.VMEM),
        scratch_shapes=[
            pltpu.VMEM((4, list_cap, block_size, block_size), jnp.bfloat16),
            pltpu.VMEM((2, list_cap, block_size, block_size), jnp.bfloat16),
            pltpu.SemaphoreType.DMA((9,)),
        ],
        compiler_params=pltpu.CompilerParams(vmem_limit_bytes=60 * 1024 * 1024),
    )(*scalars, *lists)


def shifted(value, axis, steps):
    count = lax.axis_size(axis)
    pairs = [(source, (source + steps) % count) for source in range(count)]
    return lax.ppermute(value, axis, pairs)


def on_device(left_blocks, left_rows, right_blocks, right_cols, pair_left, pair_right, pair_count):
    block_size = left_blocks.shape[-1]
    left_cap = left_blocks.shape[3]
    right_cap = right_blocks.shape[3]
    piece_count = lax.axis_size("row")
    slab_width = SLAB // piece_count
    targets = ROWS_GROUP * slab_width
    row_here = lax.axis_index("row")
    col_here = lax.axis_index("col")
    own_left = left_blocks.reshape(left_cap, block_size, block_size)
    own_right = right_blocks.reshape(right_cap, block_size, block_size)
    own_ids = left_rows.reshape(left_cap)

    ids_below = shifted(own_ids, "row", 1)
    ids_above = shifted(own_ids, "row", -1)
    ids_far = shifted(own_ids, "row", 2)
    half = left_cap // 2
    own_low, own_high = own_left[:half], own_left[half:]
    below_low = shifted(own_low, "row", 1)
    above_high = shifted(own_high, "row", -1)
    right_pair = lax.all_gather(own_right, "col")
    right_ids_pair = lax.all_gather(right_cols.reshape(right_cap), "col")
    below_low, above_high, own_low, own_high, ids_below, ids_above, ids_far = (
        lax.optimization_barrier(
            (below_low, above_high, own_low, own_high, ids_below, ids_above, ids_far)))
    below_high = shifted(own_high, "row", 1)
    above_low = shifted(own_low, "row", -1)
    far_low = shifted(below_low, "row", 1)
    far_high = shifted(above_high, "row", -1)

    slots_left_all = pair_left.reshape(piece_count, -1)
    slots_right_all = pair_right.reshape(piece_count, -1)
    counts_all = pair_count.reshape(piece_count)
    offsets = jnp.array([0, -1, 1, 2], jnp.int32)
    piece = (row_here + col_here + offsets) % piece_count
    left_id_stack = jnp.stack([own_ids, ids_below, ids_above, ids_far])
    right_id_stack = jnp.take(right_ids_pair, jnp.stack([col_here, 1 - col_here]), axis=0)
    pick = jnp.stack([1 - col_here, col_here]).astype(jnp.int32)
    scalars = (jnp.take(slots_left_all, piece, axis=0), jnp.take(slots_right_all, piece, axis=0),
               jnp.take(counts_all, piece, axis=0), left_id_stack, right_id_stack, pick)
    totals = pair_products(scalars, (own_left, below_low, below_high, above_low, above_high,
                                     far_low, far_high, own_right, right_pair), targets)
    owned = lax.psum_scatter(totals, "layer", scatter_dimension=0, tiled=True)
    return owned.reshape(1, 1, -1, block_size, block_size)


def solution(mesh):
    in_specs = (
        P("row", "col", "layer", None, None, None),
        P("row", "col", "layer", None),
        P("row", "col", "layer", None, None, None),
        P("row", "col", "layer", None),
        P("row", "col", "layer", None, None),
        P("row", "col", "layer", None, None),
        P("row", "col", "layer", None),
    )
    out_specs = P("col", "row", "layer", None, None)
    return jax.shard_map(
        on_device, mesh=mesh, in_specs=in_specs, out_specs=out_specs, check_vma=False
    )
```

```python
import jax
import jax.numpy as jnp
from jax import lax
from jax.experimental import pallas as pl
from jax.experimental.pallas import tpu as pltpu
from jax.sharding import PartitionSpec as P

SLAB = 128
ROWS_GROUP = 8
UNROLL = 16


def pair_kernel(slots_left, slots_right, counts, left_ids, right_ids, pick,
                own_left, below_low, below_high, above_low, above_high, far_low, far_high,
                own_right, right_pair, totals, left_lists, right_lists, sems):
    half = far_low.shape[0]
    slab_width = totals.shape[0] // ROWS_GROUP
    block_size = totals.shape[-1]
    copies = [
        [pltpu.make_async_copy(own_left, left_lists.at[0], sems.at[0]),
         pltpu.make_async_copy(own_right, right_lists.at[0], sems.at[1])],
        [pltpu.make_async_copy(below_low, left_lists.at[1, pl.ds(0, half)], sems.at[2]),
         pltpu.make_async_copy(below_high, left_lists.at[1, pl.ds(half, half)], sems.at[7]),
         pltpu.make_async_copy(right_pair.at[pick[0]], right_lists.at[1], sems.at[3])],
        [pltpu.make_async_copy(above_low, left_lists.at[2, pl.ds(0, half)], sems.at[4]),
         pltpu.make_async_copy(above_high, left_lists.at[2, pl.ds(half, half)], sems.at[8])],
        [pltpu.make_async_copy(far_low, left_lists.at[3, pl.ds(0, half)], sems.at[5]),
         pltpu.make_async_copy(far_high, left_lists.at[3, pl.ds(half, half)], sems.at[6])],
    ]
    for group in copies:
        for copy in group:
            copy.start()

    def clear(t, carry):
        totals[t] = jnp.zeros((block_size, block_size), jnp.float32)
        return carry

    lax.fori_loop(0, totals.shape[0], clear, 0)

    for u, v in enumerate((0, 1, 1, 0)):
        for copy in copies[u]:
            copy.wait()

        def one_term(j, u=u, v=v):
            i = slots_left[u, j]
            k = slots_right[u, j]
            t = left_ids[u, i] * slab_width + right_ids[v, k]
            term = jnp.dot(left_lists[u, i], right_lists[v, k], preferred_element_type=jnp.float32)
            return t, term

        count = counts[u]

        def add_group(g, carry, one_term=one_term, count=count):
            made = [(g * UNROLL + q, *one_term(g * UNROLL + q)) for q in range(UNROLL)]
            for j, t, term in made:
                @pl.when(j < count)
                def _(t=t, term=term):
                    totals[t] = totals[t] + term
            return carry

        lax.fori_loop(0, (count + UNROLL - 1) // UNROLL, add_group, 0)


def pair_products(scalars, lists, targets):
    own_left = lists[0]
    list_cap, block_size = own_left.shape[0], own_left.shape[-1]
    smem = pl.BlockSpec(memory_space=pltpu.SMEM)
    hbm = pl.BlockSpec(memory_space=pl.ANY)
    return pl.pallas_call(
        pair_kernel,
        out_shape=jax.ShapeDtypeStruct((targets, block_size, block_size), jnp.float32),
        in_specs=[smem] * len(scalars) + [hbm] * len(lists),
        out_specs=pl.BlockSpec(memory_space=pltpu.VMEM),
        scratch_shapes=[
            pltpu.VMEM((4, list_cap, block_size, block_size), jnp.bfloat16),
            pltpu.VMEM((2, list_cap, block_size, block_size), jnp.bfloat16),
            pltpu.SemaphoreType.DMA((9,)),
        ],
        compiler_params=pltpu.CompilerParams(vmem_limit_bytes=60 * 1024 * 1024),
    )(*scalars, *lists)


def shifted(value, axis, steps):
    count = lax.axis_size(axis)
    pairs = [(source, (source + steps) % count) for source in range(count)]
    return lax.ppermute(value, axis, pairs)


def on_device(left_blocks, left_rows, right_blocks, right_cols, pair_left, pair_right, pair_count):
    block_size = left_blocks.shape[-1]
    left_cap = left_blocks.shape[3]
    right_cap = right_blocks.shape[3]
    piece_count = lax.axis_size("row")
    slab_width = SLAB // piece_count
    targets = ROWS_GROUP * slab_width
    row_here = lax.axis_index("row")
    col_here = lax.axis_index("col")
    own_left = left_blocks.reshape(left_cap, block_size, block_size)
    own_right = right_blocks.reshape(right_cap, block_size, block_size)
    own_ids = left_rows.reshape(left_cap)

    ids_below = shifted(own_ids, "row", 1)
    ids_above = shifted(own_ids, "row", -1)
    ids_far = shifted(own_ids, "row", 2)
    half = left_cap // 2
    own_low, own_high = own_left[:half], own_left[half:]
    below_low = shifted(own_low, "row", 1)
    above_high = shifted(own_high, "row", -1)
    right_pair = lax.all_gather(own_right, "col")
    right_ids_pair = lax.all_gather(right_cols.reshape(right_cap), "col")
    below_low, above_high, own_low, own_high, ids_below, ids_above, ids_far = (
        lax.optimization_barrier(
            (below_low, above_high, own_low, own_high, ids_below, ids_above, ids_far)))
    below_high = shifted(own_high, "row", 1)
    above_low = shifted(own_low, "row", -1)
    far_low = shifted(below_low, "row", 1)
    far_high = shifted(above_high, "row", -1)

    slots_left_all = pair_left.reshape(piece_count, -1)
    slots_right_all = pair_right.reshape(piece_count, -1)
    counts_all = pair_count.reshape(piece_count)
    offsets = jnp.array([0, -1, 1, 2], jnp.int32)
    piece = (row_here + col_here + offsets) % piece_count
    left_id_stack = jnp.stack([own_ids, ids_below, ids_above, ids_far])
    right_id_stack = jnp.take(right_ids_pair, jnp.stack([col_here, 1 - col_here]), axis=0)
    pick = jnp.stack([1 - col_here, col_here]).astype(jnp.int32)
    scalars = (jnp.take(slots_left_all, piece, axis=0), jnp.take(slots_right_all, piece, axis=0),
               jnp.take(counts_all, piece, axis=0), left_id_stack, right_id_stack, pick)
    totals = pair_products(scalars, (own_left, below_low, below_high, above_low, above_high,
                                     far_low, far_high, own_right, right_pair), targets)
    owned = lax.psum_scatter(totals, "layer", scatter_dimension=0, tiled=True)
    return owned.reshape(1, 1, -1, block_size, block_size)


def solution(mesh):
    in_specs = (
        P("row", "col", "layer", None, None, None),
        P("row", "col", "layer", None),
        P("row", "col", "layer", None, None, None),
        P("row", "col", "layer", None),
        P("row", "col", "layer", None, None),
        P("row", "col", "layer", None, None),
        P("row", "col", "layer", None),
    )
    out_specs = P("col", "row", "layer", None, None)
    return jax.shard_map(
        on_device, mesh=mesh, in_specs=in_specs, out_specs=out_specs, check_vma=False
    )
```
